512 devices in a mesh: head: 4 (over x_lo, core), seq: 128 (over x_hi, z, y).
Axes of the slice: x: 4 (x_hi: 2, x_lo: 2; x = x_hi * 2 + x_lo), y: 4, z: 16, core: 2. Of those that a mesh axis runs over, the one named last changes fastest.
Arguments:
- queries: bfloat16 [32768, 32, 128], P('seq', 'head'), may hold values from -6 to 6
- normed_keys: bfloat16 [32768, 16, 128], P('seq', 'head'), may hold values from -6 to 6
- value_matrix: bfloat16 [32768, 16, 128], P('seq', 'head'), may hold values from -6 to 6
- forward_out: bfloat16 [32768, 32, 128], P('seq', 'head'), may hold values from -1.75 to 1.75
- output_gradient: bfloat16 [32768, 32, 128], P(('seq', 'head')), may hold values from -96 to 96
- row_log_total: float32 [32, 32768], P('head', 'seq'), may hold values from 6 to 8
- pair_start: int32 [32768], P('seq'), may hold values from 0 to 32256, as said below
Outputs:
- query_grad: bfloat16 [32768, 32, 128], P(('seq', 'head'))
- key_grad: bfloat16 [32768, 16, 128], P(('seq', 'head'))
- value_grad: bfloat16 [32768, 16, 128], P(('seq', 'head'))
The draws below stay inside these ranges and needn't reach their ends.
Inputs may be any that keep to these rules, and one draw needn't show every extreme that they name: pair_start[p] is the first position of the pair that holds token p: it never falls, never exceeds p, and equals p at each pair's first token; the last pair holds the final 1024 / 2 tokens, the pair before it at most 1024 tokens, and every other pair 1024 / 8 to 1024 tokens.
All inputs are finite; a program needn't handle non-finite values.
Results may differ from the reference program's by a relative error of at most 0.0059.
Values may be sent and summed in bfloat16 or wider, within the bound.
No kernel may reach another device: no remote copies, remote signals or barrier semaphores. Data moves between devices by JAX's collectives and lax.ppermute only.
A program may use at most 64 MiB of HBM per device.

```python
import jax
import jax.numpy as jnp
from jax import lax

HEAD_FEATURES = 128
QUERY_HEADCOUNT = 32
KEY_VALUE_HEADS = 16
WINDOW_LENGTH = 1024
TOKENS_PER_SHARD = 256
STREAM_TOKENS = 32768


def draw_pair_start(key, part):
    lengths = jax.random.randint(key, (STREAM_TOKENS,), WINDOW_LENGTH // 8, WINDOW_LENGTH + 1, dtype=jnp.int32)
    ends = jnp.cumsum(lengths).astype(jnp.int32)
    firsts = ends - lengths
    places = jnp.arange(STREAM_TOKENS, dtype=jnp.int32)
    which = jnp.searchsorted(ends, places, side='right')
    last_first = STREAM_TOKENS - WINDOW_LENGTH // 2
    drawn = firsts[which].astype(jnp.int32)
    return jnp.where(places >= last_first, last_first, drawn).astype(jnp.int32)


def level_of(own_key, dims, split, least, high):
    factor_of, own = 1.0, jax.random.fold_in(own_key, 6)
    for axis_at, shards_of in split:
        heights = jnp.exp(jax.random.uniform(jax.random.fold_in(own, axis_at), (shards_of,), jnp.float32, least / len(split), high / len(split)))
        factor_of = factor_of * jnp.repeat(heights, dims[axis_at] // shards_of).reshape([-1 if axis == axis_at else 1 for axis in range(len(dims))])
    return factor_of


def scatter_about(key, extent, width, bound, shards=(), held_as=jnp.bfloat16):
    entries = width * jax.random.normal(key, extent, jnp.float32)
    if shards:
        entries = entries * level_of(key, extent, shards, -0.22, 0.18)
    return jnp.clip(entries, -bound, bound).astype(held_as)


def setup_inputs(seed: int = 0) -> dict:
    seeds = jax.random.split(jax.random.key(seed), 8)
    queries = scatter_about(seeds[0], (STREAM_TOKENS, QUERY_HEADCOUNT, HEAD_FEATURES), 1.0, 6.0, ((0, 128), (1, 4)))
    normed_keys = scatter_about(seeds[1], (STREAM_TOKENS, KEY_VALUE_HEADS, HEAD_FEATURES), 1.0, 6.0, ((0, 128), (1, 4)))
    value_matrix = scatter_about(seeds[2], (STREAM_TOKENS, KEY_VALUE_HEADS, HEAD_FEATURES), 1.0, 6.0, ((0, 128), (1, 4)))
    forward_out = scatter_about(seeds[3], (STREAM_TOKENS, QUERY_HEADCOUNT, HEAD_FEATURES), 0.3, 1.75, ((0, 128), (1, 4)))
    output_gradient = scatter_about(seeds[4], (STREAM_TOKENS, QUERY_HEADCOUNT, HEAD_FEATURES), 16.0, 96.0, ((0, 512),))
    row_log_total = jnp.clip(6.0 + 2.0 * jax.random.uniform(seeds[5], (QUERY_HEADCOUNT, STREAM_TOKENS), jnp.float32) ** level_of(seeds[5], (QUERY_HEADCOUNT, STREAM_TOKENS), ((0, 4), (1, 128)), -0.2, 0.2), 6.0, 8.0)
    pair_start = draw_pair_start(jax.random.fold_in(seeds[7], 71), 0)
    return {"queries": queries, "normed_keys": normed_keys, "value_matrix": value_matrix, "forward_out": forward_out, "output_gradient": output_gradient, "row_log_total": row_log_total, "pair_start": pair_start}


score_scale = 168.0 ** -0.5


def reference(queries, normed_keys, value_matrix, forward_out, output_gradient, row_log_total, pair_start):
    group_size = QUERY_HEADCOUNT // KEY_VALUE_HEADS
    blocks = STREAM_TOKENS // TOKENS_PER_SHARD
    delta_rows = jnp.sum(forward_out.astype(jnp.float32) * output_gradient.astype(jnp.float32), axis=2)
    key_padded = jnp.concatenate([jnp.zeros((WINDOW_LENGTH, KEY_VALUE_HEADS, HEAD_FEATURES), normed_keys.dtype), normed_keys], 0)
    value_padded = jnp.concatenate([jnp.zeros((WINDOW_LENGTH, KEY_VALUE_HEADS, HEAD_FEATURES), value_matrix.dtype), value_matrix], 0)

    def one_block(carry, index):
        key_acc, value_acc = carry
        first_index = (index * TOKENS_PER_SHARD).astype(jnp.int32)
        query_block = lax.dynamic_slice_in_dim(queries, first_index, TOKENS_PER_SHARD, 0).astype(jnp.float32).reshape(TOKENS_PER_SHARD, KEY_VALUE_HEADS, group_size, HEAD_FEATURES)
        gradient_block = lax.dynamic_slice_in_dim(output_gradient, first_index, TOKENS_PER_SHARD, 0).astype(jnp.float32).reshape(TOKENS_PER_SHARD, KEY_VALUE_HEADS, group_size, HEAD_FEATURES)
        logsum_block = lax.dynamic_slice_in_dim(row_log_total, first_index, TOKENS_PER_SHARD, 1).reshape(KEY_VALUE_HEADS, group_size, TOKENS_PER_SHARD)
        delta_block = lax.dynamic_slice_in_dim(delta_rows, first_index, TOKENS_PER_SHARD, 0).T.reshape(KEY_VALUE_HEADS, group_size, TOKENS_PER_SHARD)
        start_blk = lax.dynamic_slice_in_dim(pair_start, first_index, TOKENS_PER_SHARD, 0)
        key_blk = lax.dynamic_slice_in_dim(key_padded, first_index, TOKENS_PER_SHARD + WINDOW_LENGTH, 0).astype(jnp.float32)
        value_blk = lax.dynamic_slice_in_dim(value_padded, first_index, TOKENS_PER_SHARD + WINDOW_LENGTH, 0).astype(jnp.float32)
        query_place = first_index + jnp.arange(TOKENS_PER_SHARD, dtype=jnp.int32)
        key_place = first_index - WINDOW_LENGTH + jnp.arange(TOKENS_PER_SHARD + WINDOW_LENGTH, dtype=jnp.int32)
        gap = query_place[:, None] - key_place[None, :]
        visible = (gap >= 0) & (gap < WINDOW_LENGTH) & (key_place[None, :] >= start_blk[:, None])
        scores = jnp.einsum("ikgd,jkd->kgij", query_block, key_blk) * score_scale
        probs = jnp.where(visible, jnp.exp(scores - logsum_block[..., None]), 0.0)
        probs_low = lax.optimization_barrier(probs.astype(jnp.bfloat16)).astype(jnp.float32)
        dprobs = jnp.einsum("ikgd,jkd->kgij", gradient_block, value_blk)
        dscores = probs * (dprobs - delta_block[..., None])
        dscores_low = lax.optimization_barrier(dscores.astype(jnp.bfloat16)).astype(jnp.float32)
        query_term = jnp.einsum("kgij,jkd->ikgd", dscores_low, key_blk) * score_scale
        key_term = jnp.einsum("kgij,ikgd->jkd", dscores_low, query_block)
        value_term = jnp.einsum("kgij,ikgd->jkd", probs_low, gradient_block)
        key_old = lax.dynamic_slice_in_dim(key_acc, first_index, TOKENS_PER_SHARD + WINDOW_LENGTH, 0)
        value_old = lax.dynamic_slice_in_dim(value_acc, first_index, TOKENS_PER_SHARD + WINDOW_LENGTH, 0)
        key_acc = lax.dynamic_update_slice_in_dim(key_acc, key_old + key_term, first_index, 0)
        value_acc = lax.dynamic_update_slice_in_dim(value_acc, value_old + value_term, first_index, 0)
        return (key_acc, value_acc), query_term.reshape(TOKENS_PER_SHARD, QUERY_HEADCOUNT, HEAD_FEATURES).astype(jnp.bfloat16)

    start_accumulator = jnp.zeros((STREAM_TOKENS + WINDOW_LENGTH, KEY_VALUE_HEADS, HEAD_FEATURES), jnp.float32)
    (key_acc, value_acc), query_parts = lax.scan(one_block, (start_accumulator, start_accumulator), jnp.arange(blocks, dtype=jnp.int32))
    query_grad = query_parts.reshape(STREAM_TOKENS, QUERY_HEADCOUNT, HEAD_FEATURES)
    key_grad = (key_acc[WINDOW_LENGTH:] * score_scale).astype(jnp.bfloat16)
    value_grad = value_acc[WINDOW_LENGTH:].astype(jnp.bfloat16)
    return (query_grad, key_grad, value_grad)
```

```python
import jax
import jax.numpy as jnp
from jax import lax
from jax.sharding import Mesh
from jax.sharding import PartitionSpec as P

WINDOW_LENGTH = 1024
BLOCK = 256

score_scale = 168.0 ** (-0.5)


def shifted(value, axis, by):
    size = lax.axis_size(axis)
    pairs = [(i, i + by) for i in range(size) if 0 <= i + by < size]
    return lax.ppermute(value, axis, pairs)


def band_terms(query, grad, logsum, delta, start, base, keys, values):
    tokens, group, depth = query.shape
    tiles = tokens // BLOCK
    span = WINDOW_LENGTH + BLOCK
    query_t = query.reshape(tiles, BLOCK, group, depth)
    grad_t = grad.reshape(tiles, BLOCK, group, depth)
    logsum_t = logsum.reshape(group, tiles, BLOCK).transpose(1, 0, 2)
    delta_t = delta.reshape(group, tiles, BLOCK).transpose(1, 0, 2)
    start_t = start.reshape(tiles, BLOCK)
    key_w = jnp.stack([keys[t * BLOCK : t * BLOCK + span] for t in range(tiles)])
    value_w = jnp.stack([values[t * BLOCK : t * BLOCK + span] for t in range(tiles)])
    tile_base = base + BLOCK * jnp.arange(tiles, dtype=jnp.int32)
    query_place = tile_base[:, None] + jnp.arange(BLOCK, dtype=jnp.int32)[None, :]
    key_place = tile_base[:, None] - WINDOW_LENGTH + jnp.arange(span, dtype=jnp.int32)[None, :]
    gap = query_place[:, :, None] - key_place[:, None, :]
    visible = (gap >= 0) & (gap < WINDOW_LENGTH) & (key_place[:, None, :] >= start_t[:, :, None])
    scores = (
        jnp.einsum("tigd,tjd->tgij", query_t, key_w, preferred_element_type=jnp.float32)
        * score_scale
    )
    probs = jnp.where(visible[:, None], jnp.exp(scores - logsum_t[..., None]), 0.0)
    dprobs = jnp.einsum("tigd,tjd->tgij", grad_t, value_w, preferred_element_type=jnp.float32)
    low_scores = (probs * (dprobs - delta_t[..., None])).astype(jnp.bfloat16)
    low_probs = probs.astype(jnp.bfloat16)
    query_term = jnp.einsum("tgij,tjd->tigd", low_scores, key_w, preferred_element_type=jnp.float32)
    key_w_term = jnp.einsum("tgij,tigd->tjd", low_scores, query_t, preferred_element_type=jnp.float32)
    value_w_term = jnp.einsum("tgij,tigd->tjd", low_probs, grad_t, preferred_element_type=jnp.float32)
    total = WINDOW_LENGTH + tokens
    key_term = jnp.zeros((total, depth), jnp.float32)
    value_term = jnp.zeros((total, depth), jnp.float32)
    for t in range(tiles):
        key_term = key_term.at[t * BLOCK : t * BLOCK + span].add(key_w_term[t])
        value_term = value_term.at[t * BLOCK : t * BLOCK + span].add(value_w_term[t])
    return query_term.reshape(tokens, group, depth), key_term, value_term


def on_device(
    queries, normed_keys, value_matrix, forward_out, output_gradient, row_log_total, pair_start
):
    grad_rows = lax.all_to_all(output_gradient, "head", split_axis=1, concat_axis=0, tiled=True)
    delta_rows = jnp.einsum(
        "thd,thd->ht", forward_out, grad_rows, preferred_element_type=jnp.float32
    )
    ring = lax.axis_size("sl")
    query_g = lax.all_to_all(queries, "sl", split_axis=1, concat_axis=0, tiled=True)
    grad_g = lax.all_to_all(grad_rows, "sl", split_axis=1, concat_axis=0, tiled=True)
    key_g = lax.all_to_all(normed_keys, "sl", split_axis=1, concat_axis=0, tiled=True)
    value_g = lax.all_to_all(value_matrix, "sl", split_axis=1, concat_axis=0, tiled=True)
    logsum_g = lax.all_to_all(row_log_total, "sl", split_axis=0, concat_axis=1, tiled=True)
    delta_g = lax.all_to_all(delta_rows, "sl", split_axis=0, concat_axis=1, tiled=True)
    start_g = lax.all_gather(pair_start, "sl", axis=0, tiled=True)
    tokens, group, depth = query_g.shape
    base = lax.axis_index("sh") * tokens
    key_own = key_g[:, 0]
    value_own = value_g[:, 0]
    key_far = shifted(key_own, "sh", 1)
    value_far = shifted(value_own, "sh", 1)
    keys = jnp.concatenate([key_far, key_own], axis=0)
    values = jnp.concatenate([value_far, value_own], axis=0)
    query_sum, key_sum, value_sum = band_terms(
        query_g, grad_g, logsum_g, delta_g, start_g, base, keys, values
    )
    key_back = shifted(key_sum[:WINDOW_LENGTH], "sh", -1)
    value_back = shifted(value_sum[:WINDOW_LENGTH], "sh", -1)
    key_total = key_sum[WINDOW_LENGTH:] + key_back
    value_total = value_sum[WINDOW_LENGTH:] + value_back
    query_grad = (query_sum * score_scale).astype(jnp.bfloat16)
    key_grad = (key_total * score_scale).astype(jnp.bfloat16)[:, None]
    value_grad = value_total.astype(jnp.bfloat16)[:, None]

    def back(x):
        x = lax.all_to_all(x, "sl", split_axis=0, concat_axis=1, tiled=True)
        return lax.all_to_all(x, "head", split_axis=0, concat_axis=1, tiled=True)

    return back(query_grad), back(key_grad), back(value_grad)


def solution(mesh):
    head, seq = mesh.devices.shape
    ring = WINDOW_LENGTH // BLOCK
    grouped = Mesh(mesh.devices.reshape(head, seq // ring, ring), ("head", "sh", "sl"))
    seq_axes = ("sh", "sl")
    placed = (
        P(seq_axes, "head", None),
        P(seq_axes, "head", None),
        P(seq_axes, "head", None),
        P(seq_axes, "head", None),
        P(seq_axes + ("head",), None, None),
        P("head", seq_axes),
        P(seq_axes),
    )
    out = P(seq_axes + ("head",), None, None)
    return jax.shard_map(
        on_device,
        mesh=grouped,
        in_specs=placed,
        out_specs=(out, out, out),
        check_vma=False,
    )
```

```python
import jax
import jax.numpy as jnp
from jax import lax
from jax.sharding import Mesh
from jax.sharding import PartitionSpec as P

WINDOW_LENGTH = 1024
BLOCK = 256

score_scale = 168.0 ** (-0.5)


def shifted(value, axis, by):
    size = lax.axis_size(axis)
    pairs = [(i, i + by) for i in range(size) if 0 <= i + by < size]
    return lax.ppermute(value, axis, pairs)


def band_terms(query, grad, logsum, delta, start, base, keys, values):
    tokens, group, depth = query.shape
    tiles = tokens // BLOCK
    span = WINDOW_LENGTH + BLOCK
    query_t = query.reshape(tiles, BLOCK, group, depth)
    grad_t = grad.reshape(tiles, BLOCK, group, depth)
    logsum_t = logsum.reshape(group, tiles, BLOCK).transpose(1, 0, 2)
    delta_t = delta.reshape(group, tiles, BLOCK).transpose(1, 0, 2)
    start_t = start.reshape(tiles, BLOCK)
    key_w = jnp.stack([keys[t * BLOCK : t * BLOCK + span] for t in range(tiles)])
    value_w = jnp.stack([values[t * BLOCK : t * BLOCK + span] for t in range(tiles)])
    tile_base = base + BLOCK * jnp.arange(tiles, dtype=jnp.int32)
    query_place = tile_base[:, None] + jnp.arange(BLOCK, dtype=jnp.int32)[None, :]
    key_place = tile_base[:, None] - WINDOW_LENGTH + jnp.arange(span, dtype=jnp.int32)[None, :]
    gap = query_place[:, :, None] - key_place[:, None, :]
    visible = (gap >= 0) & (gap < WINDOW_LENGTH) & (key_place[:, None, :] >= start_t[:, :, None])
    scores = (
        jnp.einsum("tigd,tjd->tgij", query_t, key_w, preferred_element_type=jnp.float32)
        * score_scale
    )
    probs = jnp.where(visible[:, None], jnp.exp(scores - logsum_t[..., None]), 0.0)
    dprobs = jnp.einsum("tigd,tjd->tgij", grad_t, value_w, preferred_element_type=jnp.float32)
    low_scores = (probs * (dprobs - delta_t[..., None])).astype(jnp.bfloat16)
    low_probs = probs.astype(jnp.bfloat16)
    query_term = jnp.einsum("tgij,tjd->tigd", low_scores, key_w, preferred_element_type=jnp.float32)
    key_w_term = jnp.einsum("tgij,tigd->tjd", low_scores, query_t, preferred_element_type=jnp.float32)
    value_w_term = jnp.einsum("tgij,tigd->tjd", low_probs, grad_t, preferred_element_type=jnp.float32)
    total = WINDOW_LENGTH + tokens
    key_term = jnp.zeros((total, depth), jnp.float32)
    value_term = jnp.zeros((total, depth), jnp.float32)
    for t in range(tiles):
        key_term = key_term.at[t * BLOCK : t * BLOCK + span].add(key_w_term[t])
        value_term = value_term.at[t * BLOCK : t * BLOCK + span].add(value_w_term[t])
    return query_term.reshape(tokens, group, depth), key_term, value_term


def on_device(
    queries, normed_keys, value_matrix, forward_out, output_gradient, row_log_total, pair_start
):
    grad_rows = lax.all_to_all(output_gradient, "head", split_axis=1, concat_axis=0, tiled=True)
    delta_rows = jnp.einsum(
        "thd,thd->ht", forward_out, grad_rows, preferred_element_type=jnp.float32
    )
    ring = lax.axis_size("sl")
    local_tokens, query_heads, depth = queries.shape
    key_heads = normed_keys.shape[1]
    group = query_heads // key_heads
    packed = jnp.concatenate(
        [
            queries.reshape(local_tokens, ring, group * key_heads // ring, depth),
            grad_rows.reshape(local_tokens, ring, group * key_heads // ring, depth),
            normed_keys.reshape(local_tokens, ring, key_heads // ring, depth),
            value_matrix.reshape(local_tokens, ring, key_heads // ring, depth),
        ],
        axis=2,
    )
    packed = lax.all_to_all(packed, "sl", split_axis=1, concat_axis=0, tiled=True)[:, 0]
    starts = jnp.broadcast_to(pair_start.astype(jnp.float32), (ring, 1, local_tokens))
    rows = jnp.concatenate(
        [
            row_log_total.reshape(ring, query_heads // ring, local_tokens),
            delta_rows.reshape(ring, query_heads // ring, local_tokens),
            starts,
        ],
        axis=1,
    )
    rows = lax.all_to_all(rows, "sl", split_axis=0, concat_axis=2, tiled=True)[0]
    heads_here = query_heads // ring
    query_g = packed[:, :heads_here]
    grad_g = packed[:, heads_here : 2 * heads_here]
    key_own = packed[:, 2 * heads_here]
    value_own = packed[:, 2 * heads_here + 1]
    logsum_g = rows[:heads_here]
    delta_g = rows[heads_here : 2 * heads_here]
    start_g = jnp.round(rows[2 * heads_here]).astype(jnp.int32)
    tokens = query_g.shape[0]
    base = lax.axis_index("sh") * tokens
    far = shifted(jnp.stack([key_own, value_own]), "sh", 1)
    keys = jnp.concatenate([far[0], key_own], axis=0)
    values = jnp.concatenate([far[1], value_own], axis=0)
    query_sum, key_sum, value_sum = band_terms(
        query_g, grad_g, logsum_g, delta_g, start_g, base, keys, values
    )
    back = shifted(
        jnp.stack([key_sum[:WINDOW_LENGTH], value_sum[:WINDOW_LENGTH]]), "sh", -1
    )
    key_total = key_sum[WINDOW_LENGTH:] + back[0]
    value_total = value_sum[WINDOW_LENGTH:] + back[1]
    query_grad = (query_sum * score_scale).astype(jnp.bfloat16)
    key_grad = (key_total * score_scale).astype(jnp.bfloat16)[:, None]
    value_grad = value_total.astype(jnp.bfloat16)[:, None]
    outs = jnp.concatenate([query_grad, key_grad, value_grad], axis=1)
    items = outs.shape[1]
    outs = lax.all_to_all(outs, "sl", split_axis=0, concat_axis=1, tiled=True)
    outs = lax.all_to_all(outs, "head", split_axis=0, concat_axis=1, tiled=True)
    head_size = lax.axis_size("head")
    outs = outs.reshape(outs.shape[0], head_size, ring, items, depth)
    rows_out = outs.shape[0]
    query_out = outs[:, :, :, :group].reshape(rows_out, -1, depth)
    key_out = outs[:, :, :, group].reshape(rows_out, -1, depth)
    value_out = outs[:, :, :, group + 1].reshape(rows_out, -1, depth)
    return query_out, key_out, value_out


def solution(mesh):
    head, seq = mesh.devices.shape
    ring = WINDOW_LENGTH // BLOCK
    grouped = Mesh(mesh.devices.reshape(head, seq // ring, ring), ("head", "sh", "sl"))
    seq_axes = ("sh", "sl")
    placed = (
        P(seq_axes, "head", None),
        P(seq_axes, "head", None),
        P(seq_axes, "head", None),
        P(seq_axes, "head", None),
        P(seq_axes + ("head",), None, None),
        P("head", seq_axes),
        P(seq_axes),
    )
    out = P(seq_axes + ("head",), None, None)
    return jax.shard_map(
        on_device,
        mesh=grouped,
        in_specs=placed,
        out_specs=(out, out, out),
        check_vma=False,
    )
```

```python
import jax
import jax.numpy as jnp
from jax import lax
from jax.sharding import Mesh
from jax.sharding import PartitionSpec as P

WINDOW_LENGTH = 1024
BLOCK = 256

score_scale = 168.0 ** (-0.5)


def shifted(value, axis, by):
    size = lax.axis_size(axis)
    pairs = [(i, i + by) for i in range(size) if 0 <= i + by < size]
    return lax.ppermute(value, axis, pairs)


def band_terms(query, grad, logsum, delta, start, base, keys, values):
    tokens, group, depth = query.shape
    tiles = tokens // BLOCK
    span = WINDOW_LENGTH + BLOCK
    query_t = query.reshape(tiles, BLOCK, group, depth)
    grad_t = grad.reshape(tiles, BLOCK, group, depth)
    logsum_t = logsum.reshape(group, tiles, BLOCK).transpose(1, 0, 2)
    delta_t = delta.reshape(group, tiles, BLOCK).transpose(1, 0, 2)
    start_t = start.reshape(tiles, BLOCK)
    key_w = jnp.stack([keys[t * BLOCK : t * BLOCK + span] for t in range(tiles)])
    value_w = jnp.stack([values[t * BLOCK : t * BLOCK + span] for t in range(tiles)])
    tile_base = base + BLOCK * jnp.arange(tiles, dtype=jnp.int32)
    query_place = tile_base[:, None] + jnp.arange(BLOCK, dtype=jnp.int32)[None, :]
    key_place = tile_base[:, None] - WINDOW_LENGTH + jnp.arange(span, dtype=jnp.int32)[None, :]
    gap = query_place[:, :, None] - key_place[:, None, :]
    visible = (gap >= 0) & (gap < WINDOW_LENGTH) & (key_place[:, None, :] >= start_t[:, :, None])
    scores = (
        jnp.einsum("tigd,tjd->tgij", query_t, key_w, preferred_element_type=jnp.float32)
        * score_scale
    )
    probs = jnp.where(visible[:, None], jnp.exp(scores - logsum_t[..., None]), 0.0)
    dprobs = jnp.einsum("tigd,tjd->tgij", grad_t, value_w, preferred_element_type=jnp.float32)
    low_scores = (probs * (dprobs - delta_t[..., None])).astype(jnp.bfloat16)
    low_probs = probs.astype(jnp.bfloat16)
    query_term = jnp.einsum("tgij,tjd->tigd", low_scores, key_w, preferred_element_type=jnp.float32)
    key_w_term = jnp.einsum("tgij,tigd->tjd", low_scores, query_t, preferred_element_type=jnp.float32)
    value_w_term = jnp.einsum("tgij,tigd->tjd", low_probs, grad_t, preferred_element_type=jnp.float32)
    total = WINDOW_LENGTH + tokens
    key_term = jnp.zeros((total, depth), jnp.float32)
    value_term = jnp.zeros((total, depth), jnp.float32)
    for t in range(tiles):
        key_term = key_term.at[t * BLOCK : t * BLOCK + span].add(key_w_term[t])
        value_term = value_term.at[t * BLOCK : t * BLOCK + span].add(value_w_term[t])
    return query_term.reshape(tokens, group, depth), key_term, value_term


def on_device(
    queries, normed_keys, value_matrix, forward_out, output_gradient, row_log_total, pair_start
):
    grad_rows = lax.all_to_all(output_gradient, "head", split_axis=1, concat_axis=0, tiled=True)
    delta_rows = jnp.einsum(
        "thd,thd->ht", forward_out, grad_rows, preferred_element_type=jnp.float32
    )
    ring = lax.axis_size("sl")
    local_tokens, query_heads, depth = queries.shape
    key_heads = normed_keys.shape[1]
    group = query_heads // key_heads
    heads_here = query_heads // ring
    kv_packed = jnp.concatenate(
        [
            normed_keys.reshape(local_tokens, ring, key_heads // ring, depth),
            value_matrix.reshape(local_tokens, ring, key_heads // ring, depth),
        ],
        axis=2,
    )
    kv_packed = lax.all_to_all(kv_packed, "sl", split_axis=1, concat_axis=0, tiled=True)[:, 0]
    key_own = kv_packed[:, 0]
    value_own = kv_packed[:, 1]
    far = shifted(kv_packed.transpose(1, 0, 2), "sh", 1)
    qd_packed = jnp.concatenate(
        [
            queries.reshape(local_tokens, ring, heads_here, depth),
            grad_rows.reshape(local_tokens, ring, heads_here, depth),
        ],
        axis=2,
    )
    qd_packed = lax.all_to_all(qd_packed, "sl", split_axis=1, concat_axis=0, tiled=True)[:, 0]
    starts = jnp.broadcast_to(pair_start.astype(jnp.float32), (ring, 1, local_tokens))
    rows = jnp.concatenate(
        [
            row_log_total.reshape(ring, heads_here, local_tokens),
            delta_rows.reshape(ring, heads_here, local_tokens),
            starts,
        ],
        axis=1,
    )
    rows = lax.all_to_all(rows, "sl", split_axis=0, concat_axis=2, tiled=True)[0]
    query_g = qd_packed[:, :heads_here]
    grad_g = qd_packed[:, heads_here:]
    logsum_g = rows[:heads_here]
    delta_g = rows[heads_here : 2 * heads_here]
    start_g = jnp.round(rows[2 * heads_here]).astype(jnp.int32)
    tokens = query_g.shape[0]
    base = lax.axis_index("sh") * tokens
    keys = jnp.concatenate([far[0], key_own], axis=0)
    values = jnp.concatenate([far[1], value_own], axis=0)
    query_sum, key_sum, value_sum = band_terms(
        query_g, grad_g, logsum_g, delta_g, start_g, base, keys, values
    )
    back = shifted(
        jnp.stack([key_sum[:WINDOW_LENGTH], value_sum[:WINDOW_LENGTH]]).astype(jnp.bfloat16),
        "sh",
        -1,
    )

    def to_tokens(x):
        x = lax.all_to_all(x, "sl", split_axis=0, concat_axis=1, tiled=True)
        return lax.all_to_all(x, "head", split_axis=0, concat_axis=1, tiled=True)

    head_size = lax.axis_size("head")
    query_grad = to_tokens((query_sum * score_scale).astype(jnp.bfloat16))
    rows_out = query_grad.shape[0]
    query_out = query_grad.reshape(rows_out, -1, depth)
    key_total = key_sum[WINDOW_LENGTH:] + back[0].astype(jnp.float32)
    value_total = value_sum[WINDOW_LENGTH:] + back[1].astype(jnp.float32)
    key_grad = (key_total * score_scale).astype(jnp.bfloat16)
    value_grad = value_total.astype(jnp.bfloat16)
    kv_out = to_tokens(jnp.stack([key_grad, value_grad], axis=1))
    kv_out = kv_out.reshape(rows_out, head_size, ring, 2, depth)
    key_out = kv_out[:, :, :, 0].reshape(rows_out, -1, depth)
    value_out = kv_out[:, :, :, 1].reshape(rows_out, -1, depth)
    return query_out, key_out, value_out


def solution(mesh):
    head, seq = mesh.devices.shape
    ring = WINDOW_LENGTH // BLOCK
    grouped = Mesh(mesh.devices.reshape(head, seq // ring, ring), ("head", "sh", "sl"))
    seq_axes = ("sh", "sl")
    placed = (
        P(seq_axes, "head", None),
        P(seq_axes, "head", None),
        P(seq_axes, "head", None),
        P(seq_axes, "head", None),
        P(seq_axes + ("head",), None, None),
        P("head", seq_axes),
        P(seq_axes),
    )
    out = P(seq_axes + ("head",), None, None)
    return jax.shard_map(
        on_device,
        mesh=grouped,
        in_specs=placed,
        out_specs=(out, out, out),
        check_vma=False,
    )
```

```python
import jax
import jax.numpy as jnp
from jax import lax
from jax.sharding import Mesh
from jax.sharding import PartitionSpec as P

WINDOW_LENGTH = 1024
BLOCK = 256

score_scale = 168.0 ** (-0.5)


def shifted(value, axis, by):
    size = lax.axis_size(axis)
    pairs = [(i, i + by) for i in range(size) if 0 <= i + by < size]
    return lax.ppermute(value, axis, pairs)


def band_terms(query, grad, logsum, delta, start, base, keys, values):
    tokens, group, depth = query.shape
    tiles = tokens // BLOCK
    span = WINDOW_LENGTH + BLOCK
    query_t = query.reshape(tiles, BLOCK, group, depth)
    grad_t = grad.reshape(tiles, BLOCK, group, depth)
    logsum_t = logsum.reshape(group, tiles, BLOCK).transpose(1, 0, 2)
    delta_t = delta.reshape(group, tiles, BLOCK).transpose(1, 0, 2)
    start_t = start.reshape(tiles, BLOCK)
    key_w = jnp.stack([keys[t * BLOCK : t * BLOCK + span] for t in range(tiles)])
    value_w = jnp.stack([values[t * BLOCK : t * BLOCK + span] for t in range(tiles)])
    tile_base = base + BLOCK * jnp.arange(tiles, dtype=jnp.int32)
    query_place = tile_base[:, None] + jnp.arange(BLOCK, dtype=jnp.int32)[None, :]
    key_place = tile_base[:, None] - WINDOW_LENGTH + jnp.arange(span, dtype=jnp.int32)[None, :]
    gap = query_place[:, :, None] - key_place[:, None, :]
    visible = (gap >= 0) & (gap < WINDOW_LENGTH) & (key_place[:, None, :] >= start_t[:, :, None])
    scores = (
        jnp.einsum("tigd,tjd->tgij", query_t, key_w, preferred_element_type=jnp.float32)
        * score_scale
    )
    probs = jnp.where(visible[:, None], jnp.exp(scores - logsum_t[..., None]), 0.0)
    dprobs = jnp.einsum("tigd,tjd->tgij", grad_t, value_w, preferred_element_type=jnp.float32)
    low_scores = (probs * (dprobs - delta_t[..., None])).astype(jnp.bfloat16)
    low_probs = probs.astype(jnp.bfloat16)
    query_term = jnp.einsum("tgij,tjd->tigd", low_scores, key_w, preferred_element_type=jnp.float32)
    key_w_term = jnp.einsum("tgij,tigd->tjd", low_scores, query_t, preferred_element_type=jnp.float32)
    value_w_term = jnp.einsum("tgij,tigd->tjd", low_probs, grad_t, preferred_element_type=jnp.float32)
    total = WINDOW_LENGTH + tokens
    key_term = jnp.zeros((total, depth), jnp.float32)
    value_term = jnp.zeros((total, depth), jnp.float32)
    for t in range(tiles):
        key_term = key_term.at[t * BLOCK : t * BLOCK + span].add(key_w_term[t])
        value_term = value_term.at[t * BLOCK : t * BLOCK + span].add(value_w_term[t])
    return query_term.reshape(tokens, group, depth), key_term, value_term


def split_three(x):
    hi = lax.reduce_precision(x, exponent_bits=8, mantissa_bits=7)
    rest = x - hi
    mid = lax.reduce_precision(rest, exponent_bits=8, mantissa_bits=7)
    lo = rest - mid
    return jnp.stack([hi, mid, lo], axis=-1).astype(jnp.bfloat16)


def join_three(parts):
    parts = parts.astype(jnp.float32)
    return (parts[..., 0] + parts[..., 1]) + parts[..., 2]


def on_device(
    queries, normed_keys, value_matrix, forward_out, output_gradient, row_log_total, pair_start
):
    ring = lax.axis_size("sl")
    head_size = lax.axis_size("head")
    local_tokens, heads_local, depth = queries.shape
    kv_local = normed_keys.shape[1]
    heads_here = heads_local // ring
    kv_here = kv_local // ring
    grad_rows = output_gradient.reshape(
        output_gradient.shape[0], head_size, ring, heads_here, depth
    ).transpose(0, 2, 1, 3, 4)
    grad_rows = grad_rows.reshape(output_gradient.shape[0], ring * head_size, heads_here, depth)
    grad_g = lax.all_to_all(
        grad_rows, ("sl", "head"), split_axis=1, concat_axis=0, tiled=True
    )[:, 0]
    logsum = row_log_total.reshape(ring, heads_here, local_tokens).transpose(2, 0, 1)
    side = jnp.concatenate(
        [
            split_three(logsum).reshape(local_tokens, ring, heads_here * 3),
            jnp.broadcast_to(
                split_three(pair_start.astype(jnp.float32))[:, None], (local_tokens, ring, 3)
            ),
        ],
        axis=2,
    )
    side = jnp.pad(side, ((0, 0), (0, 0), (0, depth - side.shape[2])))
    packed = jnp.concatenate(
        [
            queries.reshape(local_tokens, ring, heads_here, depth),
            forward_out.reshape(local_tokens, ring, heads_here, depth),
            normed_keys.reshape(local_tokens, ring, kv_here, depth),
            value_matrix.reshape(local_tokens, ring, kv_here, depth),
            side[:, :, None],
        ],
        axis=2,
    )
    packed = lax.all_to_all(packed, "sl", split_axis=1, concat_axis=0, tiled=True)[:, 0]
    query_g = packed[:, :heads_here]
    forward_g = packed[:, heads_here : 2 * heads_here]
    key_own = packed[:, 2 * heads_here]
    value_own = packed[:, 2 * heads_here + 1]
    side_g = packed[:, 2 * heads_here + 2]
    tokens = query_g.shape[0]
    logsum_g = join_three(side_g[:, : 3 * heads_here].reshape(tokens, heads_here, 3)).T
    start_g = jnp.round(join_three(side_g[:, 3 * heads_here : 3 * heads_here + 3])).astype(
        jnp.int32
    )
    delta_g = jnp.einsum("tgd,tgd->gt", forward_g, grad_g, preferred_element_type=jnp.float32)
    base = lax.axis_index("sh") * tokens
    far = shifted(jnp.stack([key_own, value_own]), "sh", 1)
    keys = jnp.concatenate([far[0], key_own], axis=0)
    values = jnp.concatenate([far[1], value_own], axis=0)
    query_sum, key_sum, value_sum = band_terms(
        query_g, grad_g, logsum_g, delta_g, start_g, base, keys, values
    )
    back = shifted(
        jnp.stack([key_sum[:WINDOW_LENGTH], value_sum[:WINDOW_LENGTH]]).astype(jnp.bfloat16),
        "sh",
        -1,
    )
    key_total = key_sum[WINDOW_LENGTH:] + back[0].astype(jnp.float32)
    value_total = value_sum[WINDOW_LENGTH:] + back[1].astype(jnp.float32)
    query_grad = (query_sum * score_scale).astype(jnp.bfloat16)
    key_grad = (key_total * score_scale).astype(jnp.bfloat16)[:, None]
    value_grad = value_total.astype(jnp.bfloat16)[:, None]
    outs = jnp.concatenate([query_grad, key_grad, value_grad], axis=1)
    items = outs.shape[1]
    outs = lax.all_to_all(outs, ("sl", "head"), split_axis=0, concat_axis=1, tiled=True)
    rows_out = outs.shape[0]
    outs = outs.reshape(rows_out, ring, head_size, items, depth).transpose(0, 2, 1, 3, 4)
    query_out = outs[:, :, :, :heads_here].reshape(rows_out, -1, depth)
    key_out = outs[:, :, :, heads_here].reshape(rows_out, -1, depth)
    value_out = outs[:, :, :, heads_here + 1].reshape(rows_out, -1, depth)
    return query_out, key_out, value_out


def solution(mesh):
    head, seq = mesh.devices.shape
    ring = WINDOW_LENGTH // BLOCK
    grouped = Mesh(mesh.devices.reshape(head, seq // ring, ring), ("head", "sh", "sl"))
    seq_axes = ("sh", "sl")
    placed = (
        P(seq_axes, "head", None),
        P(seq_axes, "head", None),
        P(seq_axes, "head", None),
        P(seq_axes, "head", None),
        P(seq_axes + ("head",), None, None),
        P("head", seq_axes),
        P(seq_axes),
    )
    out = P(seq_axes + ("head",), None, None)
    return jax.shard_map(
        on_device,
        mesh=grouped,
        in_specs=placed,
        out_specs=(out, out, out),
        check_vma=False,
    )
```

```python
import jax
import jax.numpy as jnp
from jax import lax
from jax.sharding import Mesh
from jax.sharding import PartitionSpec as P

WINDOW_LENGTH = 1024
BLOCK = 256

score_scale = 168.0 ** (-0.5)


def shifted(value, axis, by):
    size = lax.axis_size(axis)
    pairs = [(i, i + by) for i in range(size) if 0 <= i + by < size]
    return lax.ppermute(value, axis, pairs)


def band_terms(query, grad, logsum, delta, start, base, keys, values):
    group, tokens, depth = query.shape
    tiles = tokens // BLOCK
    span = WINDOW_LENGTH + BLOCK
    query_t = query.reshape(group, tiles, BLOCK, depth)
    grad_t = grad.reshape(group, tiles, BLOCK, depth)
    logsum_t = logsum.reshape(group, tiles, BLOCK).transpose(1, 0, 2)
    delta_t = delta.reshape(group, tiles, BLOCK).transpose(1, 0, 2)
    start_t = start.reshape(tiles, BLOCK)
    key_w = jnp.stack([keys[t * BLOCK : t * BLOCK + span] for t in range(tiles)])
    value_w = jnp.stack([values[t * BLOCK : t * BLOCK + span] for t in range(tiles)])
    tile_base = base + BLOCK * jnp.arange(tiles, dtype=jnp.int32)
    query_place = tile_base[:, None] + jnp.arange(BLOCK, dtype=jnp.int32)[None, :]
    key_place = tile_base[:, None] - WINDOW_LENGTH + jnp.arange(span, dtype=jnp.int32)[None, :]
    gap = query_place[:, :, None] - key_place[:, None, :]
    visible = (gap >= 0) & (gap < WINDOW_LENGTH) & (key_place[:, None, :] >= start_t[:, :, None])
    scores = (
        jnp.einsum("gtid,tjd->tgij", query_t, key_w, preferred_element_type=jnp.float32)
        * score_scale
    )
    probs = jnp.where(visible[:, None], jnp.exp(scores - logsum_t[..., None]), 0.0)
    dprobs = jnp.einsum("gtid,tjd->tgij", grad_t, value_w, preferred_element_type=jnp.float32)
    low_scores = (probs * (dprobs - delta_t[..., None])).astype(jnp.bfloat16)
    low_probs = probs.astype(jnp.bfloat16)
    query_term = jnp.einsum("tgij,tjd->tigd", low_scores, key_w, preferred_element_type=jnp.float32)
    key_w_term = jnp.einsum("tgij,gtid->tjd", low_scores, query_t, preferred_element_type=jnp.float32)
    value_w_term = jnp.einsum("tgij,gtid->tjd", low_probs, grad_t, preferred_element_type=jnp.float32)
    total = WINDOW_LENGTH + tokens
    key_term = jnp.zeros((total, depth), jnp.float32)
    value_term = jnp.zeros((total, depth), jnp.float32)
    for t in range(tiles):
        key_term = key_term.at[t * BLOCK : t * BLOCK + span].add(key_w_term[t])
        value_term = value_term.at[t * BLOCK : t * BLOCK + span].add(value_w_term[t])
    return query_term.reshape(tokens, group, depth), key_term, value_term


def split_three(x):
    hi = lax.reduce_precision(x, exponent_bits=8, mantissa_bits=7)
    rest = x - hi
    mid = lax.reduce_precision(rest, exponent_bits=8, mantissa_bits=7)
    lo = rest - mid
    return jnp.stack([hi, mid, lo], axis=-1).astype(jnp.bfloat16)


def join_three(parts):
    parts = parts.astype(jnp.float32)
    return (parts[..., 0] + parts[..., 1]) + parts[..., 2]


def on_device(
    queries, normed_keys, value_matrix, forward_out, output_gradient, row_log_total, pair_start
):
    ring = lax.axis_size("sl")
    head_size = lax.axis_size("head")
    local_tokens, heads_local, depth = queries.shape
    kv_local = normed_keys.shape[1]
    heads_here = heads_local // ring
    kv_here = kv_local // ring
    grad_rows = output_gradient.shape[0]
    grad_g = output_gradient.reshape(grad_rows, head_size, ring, heads_here, depth)
    grad_g = grad_g.transpose(2, 1, 3, 0, 4).reshape(ring * head_size, heads_here, grad_rows, depth)
    grad_g = lax.all_to_all(grad_g, ("sl", "head"), split_axis=0, concat_axis=2, tiled=True)[0]
    logsum = row_log_total.reshape(ring, heads_here, local_tokens).transpose(0, 2, 1)
    side = jnp.concatenate(
        [
            split_three(logsum).reshape(ring, local_tokens, heads_here * 3),
            jnp.broadcast_to(
                split_three(pair_start.astype(jnp.float32))[None], (ring, local_tokens, 3)
            ),
        ],
        axis=2,
    )
    side = jnp.pad(side, ((0, 0), (0, 0), (0, depth - side.shape[2])))
    kv_packed = jnp.concatenate(
        [
            normed_keys.reshape(local_tokens, ring * kv_here, depth).transpose(1, 0, 2)[:, None],
            value_matrix.reshape(local_tokens, ring * kv_here, depth).transpose(1, 0, 2)[:, None],
            side[:, None],
        ],
        axis=1,
    )
    kv_packed = lax.all_to_all(kv_packed, "sl", split_axis=0, concat_axis=2, tiled=True)[0]
    far = shifted(kv_packed[:2], "sh", 1)
    key_own = kv_packed[0]
    value_own = kv_packed[1]
    side_g = kv_packed[2]
    tokens = key_own.shape[0]
    logsum_g = join_three(side_g[:, : 3 * heads_here].reshape(tokens, heads_here, 3)).T
    start_g = jnp.round(join_three(side_g[:, 3 * heads_here : 3 * heads_here + 3])).astype(
        jnp.int32
    )
    qf_packed = jnp.concatenate(
        [
            queries.reshape(local_tokens, ring, heads_here, depth).transpose(1, 2, 0, 3),
            forward_out.reshape(local_tokens, ring, heads_here, depth).transpose(1, 2, 0, 3),
        ],
        axis=1,
    )
    qf_packed = lax.all_to_all(qf_packed, "sl", split_axis=0, concat_axis=2, tiled=True)[0]
    query_g = qf_packed[:heads_here]
    forward_g = qf_packed[heads_here:]
    delta_g = jnp.einsum("gtd,gtd->gt", forward_g, grad_g, preferred_element_type=jnp.float32)
    base = lax.axis_index("sh") * tokens
    keys = jnp.concatenate([far[0], key_own], axis=0)
    values = jnp.concatenate([far[1], value_own], axis=0)
    query_sum, key_sum, value_sum = band_terms(
        query_g, grad_g, logsum_g, delta_g, start_g, base, keys, values
    )
    back = shifted(
        jnp.stack([key_sum[:WINDOW_LENGTH], value_sum[:WINDOW_LENGTH]]).astype(jnp.bfloat16),
        "sh",
        -1,
    )

    def to_tokens(x):
        items = x.shape[1]
        x = lax.all_to_all(x, ("sl", "head"), split_axis=0, concat_axis=1, tiled=True)
        rows_out = x.shape[0]
        return x.reshape(rows_out, ring, head_size, items, depth).transpose(0, 2, 1, 3, 4)

    query_out = to_tokens((query_sum * score_scale).astype(jnp.bfloat16))
    query_out = query_out.reshape(query_out.shape[0], -1, depth)
    key_total = key_sum[WINDOW_LENGTH:] + back[0].astype(jnp.float32)
    value_total = value_sum[WINDOW_LENGTH:] + back[1].astype(jnp.float32)
    key_grad = (key_total * score_scale).astype(jnp.bfloat16)
    value_grad = value_total.astype(jnp.bfloat16)
    kv_out = to_tokens(jnp.stack([key_grad, value_grad], axis=1))
    rows_out = kv_out.shape[0]
    key_out = kv_out[:, :, :, 0].reshape(rows_out, -1, depth)
    value_out = kv_out[:, :, :, 1].reshape(rows_out, -1, depth)
    return query_out, key_out, value_out


def solution(mesh):
    head, seq = mesh.devices.shape
    ring = WINDOW_LENGTH // BLOCK
    grouped = Mesh(mesh.devices.reshape(head, seq // ring, ring), ("head", "sh", "sl"))
    seq_axes = ("sh", "sl")
    placed = (
        P(seq_axes, "head", None),
        P(seq_axes, "head", None),
        P(seq_axes, "head", None),
        P(seq_axes, "head", None),
        P(seq_axes + ("head",), None, None),
        P("head", seq_axes),
        P(seq_axes),
    )
    out = P(seq_axes + ("head",), None, None)
    return jax.shard_map(
        on_device,
        mesh=grouped,
        in_specs=placed,
        out_specs=(out, out, out),
        check_vma=False,
    )
```

```python
import jax
import jax.numpy as jnp
from jax import lax
from jax.sharding import Mesh
from jax.sharding import PartitionSpec as P

WINDOW_LENGTH = 1024
BLOCK = 256

score_scale = 168.0 ** (-0.5)


def shifted(value, axis, by):
    size = lax.axis_size(axis)
    pairs = [(i, i + by) for i in range(size) if 0 <= i + by < size]
    return lax.ppermute(value, axis, pairs)


def band_terms(query, grad, logsum, delta, start, base, keys, values):
    group, tokens, depth = query.shape
    tiles = tokens // BLOCK
    span = WINDOW_LENGTH + BLOCK
    query_t = query.reshape(group, tiles, BLOCK, depth)
    grad_t = grad.reshape(group, tiles, BLOCK, depth)
    logsum_t = logsum.reshape(group, tiles, BLOCK).transpose(1, 0, 2)
    delta_t = delta.reshape(group, tiles, BLOCK).transpose(1, 0, 2)
    start_t = start.reshape(tiles, BLOCK)
    key_w = jnp.stack([keys[t * BLOCK : t * BLOCK + span] for t in range(tiles)])
    value_w = jnp.stack([values[t * BLOCK : t * BLOCK + span] for t in range(tiles)])
    tile_base = base + BLOCK * jnp.arange(tiles, dtype=jnp.int32)
    query_place = tile_base[:, None] + jnp.arange(BLOCK, dtype=jnp.int32)[None, :]
    key_place = tile_base[:, None] - WINDOW_LENGTH + jnp.arange(span, dtype=jnp.int32)[None, :]
    gap = query_place[:, :, None] - key_place[:, None, :]
    visible = (gap >= 0) & (gap < WINDOW_LENGTH) & (key_place[:, None, :] >= start_t[:, :, None])
    scores = (
        jnp.einsum("gtid,tjd->tgij", query_t, key_w, preferred_element_type=jnp.float32)
        * score_scale
    )
    probs = jnp.where(visible[:, None], jnp.exp(scores - logsum_t[..., None]), 0.0)
    dprobs = jnp.einsum("gtid,tjd->tgij", grad_t, value_w, preferred_element_type=jnp.float32)
    low_scores = (probs * (dprobs - delta_t[..., None])).astype(jnp.bfloat16)
    low_probs = probs.astype(jnp.bfloat16)
    query_term = jnp.einsum("tgij,tjd->tigd", low_scores, key_w, preferred_element_type=jnp.float32)
    key_w_term = jnp.einsum("tgij,gtid->tjd", low_scores, query_t, preferred_element_type=jnp.float32)
    value_w_term = jnp.einsum("tgij,gtid->tjd", low_probs, grad_t, preferred_element_type=jnp.float32)
    total = WINDOW_LENGTH + tokens
    key_term = jnp.zeros((total, depth), jnp.float32)
    value_term = jnp.zeros((total, depth), jnp.float32)
    for t in range(tiles):
        key_term = key_term.at[t * BLOCK : t * BLOCK + span].add(key_w_term[t])
        value_term = value_term.at[t * BLOCK : t * BLOCK + span].add(value_w_term[t])
    return query_term.reshape(tokens, group, depth), key_term, value_term


def split_three(x):
    hi = lax.reduce_precision(x, exponent_bits=8, mantissa_bits=7)
    rest = x - hi
    mid = lax.reduce_precision(rest, exponent_bits=8, mantissa_bits=7)
    lo = rest - mid
    return jnp.stack([hi, mid, lo], axis=-1).astype(jnp.bfloat16)


def join_three(parts):
    parts = parts.astype(jnp.float32)
    return (parts[..., 0] + parts[..., 1]) + parts[..., 2]


def on_device(
    queries, normed_keys, value_matrix, forward_out, output_gradient, row_log_total, pair_start
):
    ring = lax.axis_size("sl")
    head_size = lax.axis_size("head")
    local_tokens, heads_local, depth = queries.shape
    kv_local = normed_keys.shape[1]
    heads_here = heads_local // ring
    kv_here = kv_local // ring
    grad_rows = output_gradient.shape[0]
    grad_g = output_gradient.reshape(grad_rows, head_size, ring, heads_here, depth)
    grad_g = grad_g.transpose(2, 1, 3, 0, 4).reshape(ring * head_size, heads_here, grad_rows, depth)
    logsum = row_log_total.reshape(ring, heads_here, local_tokens).transpose(0, 2, 1)
    side = jnp.concatenate(
        [
            split_three(logsum).reshape(ring, local_tokens, heads_here * 3),
            jnp.broadcast_to(
                split_three(pair_start.astype(jnp.float32))[None], (ring, local_tokens, 3)
            ),
        ],
        axis=2,
    )
    side = jnp.pad(side, ((0, 0), (0, 0), (0, depth - side.shape[2])))
    kv_packed = jnp.concatenate(
        [
            normed_keys.reshape(local_tokens, ring * kv_here, depth).transpose(1, 0, 2)[:, None],
            value_matrix.reshape(local_tokens, ring * kv_here, depth).transpose(1, 0, 2)[:, None],
            side[:, None],
        ],
        axis=1,
    )
    kv_packed = lax.all_to_all(kv_packed, "sl", split_axis=0, concat_axis=2, tiled=True)[0]
    far = shifted(kv_packed[:2], "sh", 1)
    grad_g, kv_packed = lax.optimization_barrier((grad_g, kv_packed))
    grad_g = lax.all_to_all(grad_g, ("sl", "head"), split_axis=0, concat_axis=2, tiled=True)[0]
    key_own = kv_packed[0]
    value_own = kv_packed[1]
    side_g = kv_packed[2]
    tokens = key_own.shape[0]
    logsum_g = join_three(side_g[:, : 3 * heads_here].reshape(tokens, heads_here, 3)).T
    start_g = jnp.round(join_three(side_g[:, 3 * heads_here : 3 * heads_here + 3])).astype(
        jnp.int32
    )
    qf_packed = jnp.concatenate(
        [
            queries.reshape(local_tokens, ring, heads_here, depth).transpose(1, 2, 0, 3),
            forward_out.reshape(local_tokens, ring, heads_here, depth).transpose(1, 2, 0, 3),
        ],
        axis=1,
    )
    qf_packed = lax.all_to_all(qf_packed, "sl", split_axis=0, concat_axis=2, tiled=True)[0]
    query_g = qf_packed[:heads_here]
    forward_g = qf_packed[heads_here:]
    delta_g = jnp.einsum("gtd,gtd->gt", forward_g, grad_g, preferred_element_type=jnp.float32)
    base = lax.axis_index("sh") * tokens
    keys = jnp.concatenate([far[0], key_own], axis=0)
    values = jnp.concatenate([far[1], value_own], axis=0)
    query_sum, key_sum, value_sum = band_terms(
        query_g, grad_g, logsum_g, delta_g, start_g, base, keys, values
    )
    back = shifted(
        jnp.stack([key_sum[:WINDOW_LENGTH], value_sum[:WINDOW_LENGTH]]).astype(jnp.bfloat16),
        "sh",
        -1,
    )

    def to_tokens(x):
        items = x.shape[1]
        x = lax.all_to_all(x, ("sl", "head"), split_axis=0, concat_axis=1, tiled=True)
        rows_out = x.shape[0]
        return x.reshape(rows_out, ring, head_size, items, depth).transpose(0, 2, 1, 3, 4)

    query_out = to_tokens((query_sum * score_scale).astype(jnp.bfloat16))
    query_out = query_out.reshape(query_out.shape[0], -1, depth)
    key_total = key_sum[WINDOW_LENGTH:] + back[0].astype(jnp.float32)
    value_total = value_sum[WINDOW_LENGTH:] + back[1].astype(jnp.float32)
    key_grad = (key_total * score_scale).astype(jnp.bfloat16)
    value_grad = value_total.astype(jnp.bfloat16)
    kv_out = to_tokens(jnp.stack([key_grad, value_grad], axis=1))
    rows_out = kv_out.shape[0]
    key_out = kv_out[:, :, :, 0].reshape(rows_out, -1, depth)
    value_out = kv_out[:, :, :, 1].reshape(rows_out, -1, depth)
    return query_out, key_out, value_out


def solution(mesh):
    head, seq = mesh.devices.shape
    ring = WINDOW_LENGTH // BLOCK
    grouped = Mesh(mesh.devices.reshape(head, seq // ring, ring), ("head", "sh", "sl"))
    seq_axes = ("sh", "sl")
    placed = (
        P(seq_axes, "head", None),
        P(seq_axes, "head", None),
        P(seq_axes, "head", None),
        P(seq_axes, "head", None),
        P(seq_axes + ("head",), None, None),
        P("head", seq_axes),
        P(seq_axes),
    )
    out = P(seq_axes + ("head",), None, None)
    return jax.shard_map(
        on_device,
        mesh=grouped,
        in_specs=placed,
        out_specs=(out, out, out),
        check_vma=False,
    )
```

```python
import jax
import jax.numpy as jnp
from jax import lax
from jax.experimental import pallas as pl
from jax.sharding import Mesh
from jax.sharding import PartitionSpec as P

WINDOW_LENGTH = 1024
BLOCK = 256

score_scale = 168.0 ** (-0.5)


def shifted(value, axis, by):
    size = lax.axis_size(axis)
    pairs = [(i, i + by) for i in range(size) if 0 <= i + by < size]
    return lax.ppermute(value, axis, pairs)


def band_terms(query, grad, logsum, delta, start, base, keys, values):
    group, tokens, depth = query.shape
    tiles = tokens // BLOCK
    span = WINDOW_LENGTH + BLOCK
    query_t = query.reshape(group, tiles, BLOCK, depth)
    grad_t = grad.reshape(group, tiles, BLOCK, depth)
    logsum_t = logsum.reshape(group, tiles, BLOCK).transpose(1, 0, 2)
    delta_t = delta.reshape(group, tiles, BLOCK).transpose(1, 0, 2)
    start_t = start.reshape(tiles, BLOCK)
    key_w = jnp.stack([keys[t * BLOCK : t * BLOCK + span] for t in range(tiles)])
    value_w = jnp.stack([values[t * BLOCK : t * BLOCK + span] for t in range(tiles)])
    tile_base = base + BLOCK * jnp.arange(tiles, dtype=jnp.int32)
    query_place = tile_base[:, None] + jnp.arange(BLOCK, dtype=jnp.int32)[None, :]
    key_place = tile_base[:, None] - WINDOW_LENGTH + jnp.arange(span, dtype=jnp.int32)[None, :]
    gap = query_place[:, :, None] - key_place[:, None, :]
    visible = (gap >= 0) & (gap < WINDOW_LENGTH) & (key_place[:, None, :] >= start_t[:, :, None])
    scores = (
        jnp.einsum("gtid,tjd->tgij", query_t, key_w, preferred_element_type=jnp.float32)
        * score_scale
    )
    probs = jnp.where(visible[:, None], jnp.exp(scores - logsum_t[..., None]), 0.0)
    dprobs = jnp.einsum("gtid,tjd->tgij", grad_t, value_w, preferred_element_type=jnp.float32)
    low_scores = (probs * (dprobs - delta_t[..., None])).astype(jnp.bfloat16)
    low_probs = probs.astype(jnp.bfloat16)
    query_term = jnp.einsum("tgij,tjd->tigd", low_scores, key_w, preferred_element_type=jnp.float32)
    key_w_term = jnp.einsum("tgij,gtid->tjd", low_scores, query_t, preferred_element_type=jnp.float32)
    value_w_term = jnp.einsum("tgij,gtid->tjd", low_probs, grad_t, preferred_element_type=jnp.float32)
    total = WINDOW_LENGTH + tokens
    key_term = jnp.zeros((total, depth), jnp.float32)
    value_term = jnp.zeros((total, depth), jnp.float32)
    for t in range(tiles):
        key_term = key_term.at[t * BLOCK : t * BLOCK + span].add(key_w_term[t])
        value_term = value_term.at[t * BLOCK : t * BLOCK + span].add(value_w_term[t])
    return query_term.reshape(tokens, group, depth), key_term, value_term


def band_kernel(q_ref, g_ref, lse_ref, dl_ref, ps_ref, k_ref, v_ref, dq_ref, dk_ref, dv_ref):
    heads, tokens, depth = q_ref.shape
    tiles = tokens // BLOCK
    reach = WINDOW_LENGTH // BLOCK + 1
    dk_ref[...] = jnp.zeros(dk_ref.shape, jnp.float32)
    dv_ref[...] = jnp.zeros(dv_ref.shape, jnp.float32)
    last = (((0,), (0,)), ((), ()))
    cross = (((1,), (1,)), ((), ()))
    row = lax.broadcasted_iota(jnp.int32, (BLOCK, BLOCK), 0)
    col = lax.broadcasted_iota(jnp.int32, (BLOCK, BLOCK), 1)

    def one_tile(t, carry):
        first = pl.multiple_of(t * BLOCK, BLOCK)
        starts = ps_ref[pl.ds(first, BLOCK), :]
        for h in range(heads):
            query = q_ref[h, pl.ds(first, BLOCK), :]
            grad = g_ref[h, pl.ds(first, BLOCK), :]
            logsum = lse_ref[h, pl.ds(first, BLOCK), :]
            delta = dl_ref[h, pl.ds(first, BLOCK), :]
            query_acc = jnp.zeros((BLOCK, depth), jnp.float32)
            for b in range(reach):
                key_first = pl.multiple_of((t + b) * BLOCK, BLOCK)
                key = k_ref[pl.ds(key_first, BLOCK), :]
                value = v_ref[pl.ds(key_first, BLOCK), :]
                scores = (
                    lax.dot_general(query, key, cross, preferred_element_type=jnp.float32)
                    * score_scale
                )
                gap = row - col + (WINDOW_LENGTH - b * BLOCK)
                visible = (gap >= 0) & (gap < WINDOW_LENGTH) & (col + key_first >= starts)
                probs = jnp.where(visible, jnp.exp(scores - logsum), 0.0)
                dprobs = lax.dot_general(grad, value, cross, preferred_element_type=jnp.float32)
                low_scores = (probs * (dprobs - delta)).astype(jnp.bfloat16)
                query_acc = query_acc + jnp.dot(
                    low_scores, key, preferred_element_type=jnp.float32
                )
                dk_ref[pl.ds(key_first, BLOCK), :] += lax.dot_general(
                    low_scores, query, last, preferred_element_type=jnp.float32
                )
                dv_ref[pl.ds(key_first, BLOCK), :] += lax.dot_general(
                    probs.astype(jnp.bfloat16), grad, last, preferred_element_type=jnp.float32
                )
            dq_ref[h, pl.ds(first, BLOCK), :] = query_acc
        return carry

    lax.fori_loop(0, tiles, one_tile, 0)


def band_pallas(query, grad, logsum, delta, start, base, keys, values):
    group, tokens, depth = query.shape
    total = keys.shape[0]
    start_rel = (start - base + WINDOW_LENGTH)[:, None]
    dq, dk, dv = pl.pallas_call(
        band_kernel,
        out_shape=(
            jax.ShapeDtypeStruct((group, tokens, depth), jnp.float32),
            jax.ShapeDtypeStruct((total, depth), jnp.float32),
            jax.ShapeDtypeStruct((total, depth), jnp.float32),
        ),
    )(query, grad, logsum[..., None], delta[..., None], start_rel, keys, values)
    return dq.transpose(1, 0, 2), dk, dv


def split_three(x):
    hi = lax.reduce_precision(x, exponent_bits=8, mantissa_bits=7)
    rest = x - hi
    mid = lax.reduce_precision(rest, exponent_bits=8, mantissa_bits=7)
    lo = rest - mid
    return jnp.stack([hi, mid, lo], axis=-1).astype(jnp.bfloat16)


def join_three(parts):
    parts = parts.astype(jnp.float32)
    return (parts[..., 0] + parts[..., 1]) + parts[..., 2]


def on_device(
    queries, normed_keys, value_matrix, forward_out, output_gradient, row_log_total, pair_start
):
    ring = lax.axis_size("sl")
    head_size = lax.axis_size("head")
    local_tokens, heads_local, depth = queries.shape
    kv_local = normed_keys.shape[1]
    heads_here = heads_local // ring
    kv_here = kv_local // ring
    grad_rows = output_gradient.shape[0]
    grad_g = output_gradient.reshape(grad_rows, head_size, ring, heads_here, depth)
    grad_g = grad_g.transpose(2, 1, 3, 0, 4).reshape(ring * head_size, heads_here, grad_rows, depth)
    logsum = row_log_total.reshape(ring, heads_here, local_tokens).transpose(0, 2, 1)
    side = jnp.concatenate(
        [
            split_three(logsum).reshape(ring, local_tokens, heads_here * 3),
            jnp.broadcast_to(
                split_three(pair_start.astype(jnp.float32))[None], (ring, local_tokens, 3)
            ),
        ],
        axis=2,
    )
    side = jnp.pad(side, ((0, 0), (0, 0), (0, depth - side.shape[2])))
    kv_packed = jnp.concatenate(
        [
            normed_keys.reshape(local_tokens, ring * kv_here, depth).transpose(1, 0, 2)[:, None],
            value_matrix.reshape(local_tokens, ring * kv_here, depth).transpose(1, 0, 2)[:, None],
            side[:, None],
        ],
        axis=1,
    )
    kv_packed = lax.all_to_all(kv_packed, "sl", split_axis=0, concat_axis=2, tiled=True)[0]
    far = shifted(kv_packed[:2], "sh", 1)
    grad_g, kv_packed = lax.optimization_barrier((grad_g, kv_packed))
    grad_g = lax.all_to_all(grad_g, ("sl", "head"), split_axis=0, concat_axis=2, tiled=True)[0]
    key_own = kv_packed[0]
    value_own = kv_packed[1]
    side_g = kv_packed[2]
    tokens = key_own.shape[0]
    logsum_g = join_three(side_g[:, : 3 * heads_here].reshape(tokens, heads_here, 3)).T
    start_g = jnp.round(join_three(side_g[:, 3 * heads_here : 3 * heads_here + 3])).astype(
        jnp.int32
    )
    qf_packed = jnp.concatenate(
        [
            queries.reshape(local_tokens, ring, heads_here, depth).transpose(1, 2, 0, 3),
            forward_out.reshape(local_tokens, ring, heads_here, depth).transpose(1, 2, 0, 3),
        ],
        axis=1,
    )
    qf_packed = lax.all_to_all(qf_packed, "sl", split_axis=0, concat_axis=2, tiled=True)[0]
    query_g = qf_packed[:heads_here]
    forward_g = qf_packed[heads_here:]
    delta_g = jnp.einsum("gtd,gtd->gt", forward_g, grad_g, preferred_element_type=jnp.float32)
    base = lax.axis_index("sh") * tokens
    keys = jnp.concatenate([far[0], key_own], axis=0)
    values = jnp.concatenate([far[1], value_own], axis=0)
    query_sum, key_sum, value_sum = band_pallas(
        query_g, grad_g, logsum_g, delta_g, start_g, base, keys, values
    )
    back = shifted(
        jnp.stack([key_sum[:WINDOW_LENGTH], value_sum[:WINDOW_LENGTH]]).astype(jnp.bfloat16),
        "sh",
        -1,
    )

    def to_tokens(x):
        items = x.shape[1]
        x = lax.all_to_all(x, ("sl", "head"), split_axis=0, concat_axis=1, tiled=True)
        rows_out = x.shape[0]
        return x.reshape(rows_out, ring, head_size, items, depth).transpose(0, 2, 1, 3, 4)

    query_out = to_tokens((query_sum * score_scale).astype(jnp.bfloat16))
    query_out = query_out.reshape(query_out.shape[0], -1, depth)
    key_total = key_sum[WINDOW_LENGTH:] + back[0].astype(jnp.float32)
    value_total = value_sum[WINDOW_LENGTH:] + back[1].astype(jnp.float32)
    key_grad = (key_total * score_scale).astype(jnp.bfloat16)
    value_grad = value_total.astype(jnp.bfloat16)
    kv_out = to_tokens(jnp.stack([key_grad, value_grad], axis=1))
    rows_out = kv_out.shape[0]
    key_out = kv_out[:, :, :, 0].reshape(rows_out, -1, depth)
    value_out = kv_out[:, :, :, 1].reshape(rows_out, -1, depth)
    return query_out, key_out, value_out


def solution(mesh):
    head, seq = mesh.devices.shape
    ring = WINDOW_LENGTH // BLOCK
    grouped = Mesh(mesh.devices.reshape(head, seq // ring, ring), ("head", "sh", "sl"))
    seq_axes = ("sh", "sl")
    placed = (
        P(seq_axes, "head", None),
        P(seq_axes, "head", None),
        P(seq_axes, "head", None),
        P(seq_axes, "head", None),
        P(seq_axes + ("head",), None, None),
        P("head", seq_axes),
        P(seq_axes),
    )
    out = P(seq_axes + ("head",), None, None)
    return jax.shard_map(
        on_device,
        mesh=grouped,
        in_specs=placed,
        out_specs=(out, out, out),
        check_vma=False,
    )
```

```python
from functools import partial

import jax
import jax.numpy as jnp
from jax import lax
from jax.experimental import pallas as pl
from jax.sharding import Mesh
from jax.sharding import PartitionSpec as P

WINDOW_LENGTH = 1024
BLOCK = 256

score_scale = 168.0 ** (-0.5)


def shifted(value, axis, by):
    size = lax.axis_size(axis)
    pairs = [(i, i + by) for i in range(size) if 0 <= i + by < size]
    return lax.ppermute(value, axis, pairs)


def band_terms(query, grad, logsum, delta, start, base, keys, values):
    group, tokens, depth = query.shape
    tiles = tokens // BLOCK
    span = WINDOW_LENGTH + BLOCK
    query_t = query.reshape(group, tiles, BLOCK, depth)
    grad_t = grad.reshape(group, tiles, BLOCK, depth)
    logsum_t = logsum.reshape(group, tiles, BLOCK).transpose(1, 0, 2)
    delta_t = delta.reshape(group, tiles, BLOCK).transpose(1, 0, 2)
    start_t = start.reshape(tiles, BLOCK)
    key_w = jnp.stack([keys[t * BLOCK : t * BLOCK + span] for t in range(tiles)])
    value_w = jnp.stack([values[t * BLOCK : t * BLOCK + span] for t in range(tiles)])
    tile_base = base + BLOCK * jnp.arange(tiles, dtype=jnp.int32)
    query_place = tile_base[:, None] + jnp.arange(BLOCK, dtype=jnp.int32)[None, :]
    key_place = tile_base[:, None] - WINDOW_LENGTH + jnp.arange(span, dtype=jnp.int32)[None, :]
    gap = query_place[:, :, None] - key_place[:, None, :]
    visible = (gap >= 0) & (gap < WINDOW_LENGTH) & (key_place[:, None, :] >= start_t[:, :, None])
    scores = (
        jnp.einsum("gtid,tjd->tgij", query_t, key_w, preferred_element_type=jnp.float32)
        * score_scale
    )
    probs = jnp.where(visible[:, None], jnp.exp(scores - logsum_t[..., None]), 0.0)
    dprobs = jnp.einsum("gtid,tjd->tgij", grad_t, value_w, preferred_element_type=jnp.float32)
    low_scores = (probs * (dprobs - delta_t[..., None])).astype(jnp.bfloat16)
    low_probs = probs.astype(jnp.bfloat16)
    query_term = jnp.einsum("tgij,tjd->tigd", low_scores, key_w, preferred_element_type=jnp.float32)
    key_w_term = jnp.einsum("tgij,gtid->tjd", low_scores, query_t, preferred_element_type=jnp.float32)
    value_w_term = jnp.einsum("tgij,gtid->tjd", low_probs, grad_t, preferred_element_type=jnp.float32)
    total = WINDOW_LENGTH + tokens
    key_term = jnp.zeros((total, depth), jnp.float32)
    value_term = jnp.zeros((total, depth), jnp.float32)
    for t in range(tiles):
        key_term = key_term.at[t * BLOCK : t * BLOCK + span].add(key_w_term[t])
        value_term = value_term.at[t * BLOCK : t * BLOCK + span].add(value_w_term[t])
    return query_term.reshape(tokens, group, depth), key_term, value_term


def band_kernel(halo, q_ref, g_ref, lse_ref, dl_ref, ps_ref, k_ref, v_ref, dq_ref, dk_ref, dv_ref):
    heads, tokens, depth = q_ref.shape
    tiles = tokens // BLOCK
    reach = WINDOW_LENGTH // BLOCK
    dk_ref[...] = jnp.zeros(dk_ref.shape, jnp.float32)
    dv_ref[...] = jnp.zeros(dv_ref.shape, jnp.float32)
    last = (((0,), (0,)), ((), ()))
    cross = (((1,), (1,)), ((), ()))
    gap = lax.broadcasted_iota(jnp.int32, (BLOCK, BLOCK), 0) - lax.broadcasted_iota(
        jnp.int32, (BLOCK, BLOCK), 1
    )
    col = lax.broadcasted_iota(jnp.int32, (BLOCK, BLOCK), 1)
    for t in range(tiles):
        rows = slice(t * BLOCK, (t + 1) * BLOCK)
        if halo:
            blocks = [(b, t + b) for b in range(reach - t)]
        else:
            blocks = [(b, t + b - reach) for b in range(reach - t, reach + 1)]
        starts = ps_ref[rows, :]
        for h in range(heads):
            query = q_ref[h, rows, :]
            grad = g_ref[h, rows, :]
            logsum = lse_ref[h, rows, :]
            delta = dl_ref[h, rows, :]
            query_acc = jnp.zeros((BLOCK, depth), jnp.float32)
            for b, kb in blocks:
                keys_at = slice(kb * BLOCK, (kb + 1) * BLOCK)
                key = k_ref[keys_at, :]
                value = v_ref[keys_at, :]
                scores = (
                    lax.dot_general(query, key, cross, preferred_element_type=jnp.float32)
                    * score_scale
                )
                key_first = kb * BLOCK + (0 if halo else WINDOW_LENGTH)
                visible = col >= starts - key_first
                if b == 0:
                    visible = visible & (gap < 0)
                if b == reach:
                    visible = visible & (gap >= 0)
                probs = jnp.where(visible, jnp.exp(scores - logsum), 0.0)
                dprobs = lax.dot_general(grad, value, cross, preferred_element_type=jnp.float32)
                low_scores = (probs * (dprobs - delta)).astype(jnp.bfloat16)
                query_acc = query_acc + jnp.dot(
                    low_scores, key, preferred_element_type=jnp.float32
                )
                dk_ref[keys_at, :] += lax.dot_general(
                    low_scores, query, last, preferred_element_type=jnp.float32
                )
                dv_ref[keys_at, :] += lax.dot_general(
                    probs.astype(jnp.bfloat16), grad, last, preferred_element_type=jnp.float32
                )
            dq_ref[h, rows, :] = query_acc


def band_part(halo, query, grad, logsum, delta, start_rel, keys, values):
    group, tokens, depth = query.shape
    total = keys.shape[0]
    return pl.pallas_call(
        partial(band_kernel, halo),
        out_shape=(
            jax.ShapeDtypeStruct((group, tokens, depth), jnp.float32),
            jax.ShapeDtypeStruct((total, depth), jnp.float32),
            jax.ShapeDtypeStruct((total, depth), jnp.float32),
        ),
    )(query, grad, logsum[..., None], delta[..., None], start_rel, keys, values)


def split_three(x):
    hi = lax.reduce_precision(x, exponent_bits=8, mantissa_bits=7)
    rest = x - hi
    mid = lax.reduce_precision(rest, exponent_bits=8, mantissa_bits=7)
    lo = rest - mid
    return jnp.stack([hi, mid, lo], axis=-1).astype(jnp.bfloat16)


def join_three(parts):
    parts = parts.astype(jnp.float32)
    return (parts[..., 0] + parts[..., 1]) + parts[..., 2]


def on_device(
    queries, normed_keys, value_matrix, forward_out, output_gradient, row_log_total, pair_start
):
    ring = lax.axis_size("sl")
    head_size = lax.axis_size("head")
    local_tokens, heads_local, depth = queries.shape
    kv_local = normed_keys.shape[1]
    heads_here = heads_local // ring
    kv_here = kv_local // ring
    grad_rows = output_gradient.shape[0]
    grad_g = output_gradient.reshape(grad_rows, head_size, ring, heads_here, depth)
    grad_g = grad_g.transpose(2, 1, 3, 0, 4).reshape(ring * head_size, heads_here, grad_rows, depth)
    logsum = row_log_total.reshape(ring, heads_here, local_tokens).transpose(0, 2, 1)
    side = jnp.concatenate(
        [
            split_three(logsum).reshape(ring, local_tokens, heads_here * 3),
            jnp.broadcast_to(
                split_three(pair_start.astype(jnp.float32))[None], (ring, local_tokens, 3)
            ),
        ],
        axis=2,
    )
    side = jnp.pad(side, ((0, 0), (0, 0), (0, depth - side.shape[2])))
    kv_packed = jnp.concatenate(
        [
            normed_keys.reshape(local_tokens, ring * kv_here, depth).transpose(1, 0, 2)[:, None],
            value_matrix.reshape(local_tokens, ring * kv_here, depth).transpose(1, 0, 2)[:, None],
            side[:, None],
        ],
        axis=1,
    )
    kv_packed = lax.all_to_all(kv_packed, "sl", split_axis=0, concat_axis=2, tiled=True)[0]
    far = shifted(kv_packed[:2], "sh", 1)
    grad_g, kv_packed = lax.optimization_barrier((grad_g, kv_packed))
    grad_g = lax.all_to_all(grad_g, ("sl", "head"), split_axis=0, concat_axis=2, tiled=True)[0]
    key_own = kv_packed[0]
    value_own = kv_packed[1]
    side_g = kv_packed[2]
    tokens = key_own.shape[0]
    logsum_g = join_three(side_g[:, : 3 * heads_here].reshape(tokens, heads_here, 3)).T
    start_g = jnp.round(join_three(side_g[:, 3 * heads_here : 3 * heads_here + 3])).astype(
        jnp.int32
    )
    qf_packed = jnp.concatenate(
        [
            queries.reshape(local_tokens, ring, heads_here, depth).transpose(1, 2, 0, 3),
            forward_out.reshape(local_tokens, ring, heads_here, depth).transpose(1, 2, 0, 3),
        ],
        axis=1,
    )
    qf_packed = lax.all_to_all(qf_packed, "sl", split_axis=0, concat_axis=2, tiled=True)[0]
    query_g = qf_packed[:heads_here]
    forward_g = qf_packed[heads_here:]
    delta_g = jnp.einsum("gtd,gtd->gt", forward_g, grad_g, preferred_element_type=jnp.float32)
    base = lax.axis_index("sh") * tokens
    start_rel = (start_g - base + WINDOW_LENGTH)[:, None]
    query_far, key_far, value_far = band_part(
        True, query_g, grad_g, logsum_g, delta_g, start_rel, far[0], far[1]
    )
    back = shifted(jnp.stack([key_far, value_far]).astype(jnp.bfloat16), "sh", -1)
    query_g, key_far = lax.optimization_barrier((query_g, key_far))
    query_own, key_sum, value_sum = band_part(
        False, query_g, grad_g, logsum_g, delta_g, start_rel, key_own, value_own
    )
    query_sum = (query_far + query_own).transpose(1, 0, 2)

    def to_tokens(x):
        items = x.shape[1]
        x = lax.all_to_all(x, ("sl", "head"), split_axis=0, concat_axis=1, tiled=True)
        rows_out = x.shape[0]
        return x.reshape(rows_out, ring, head_size, items, depth).transpose(0, 2, 1, 3, 4)

    query_out = to_tokens((query_sum * score_scale).astype(jnp.bfloat16))
    query_out = query_out.reshape(query_out.shape[0], -1, depth)
    key_total = key_sum + back[0].astype(jnp.float32)
    value_total = value_sum + back[1].astype(jnp.float32)
    key_grad = (key_total * score_scale).astype(jnp.bfloat16)
    value_grad = value_total.astype(jnp.bfloat16)
    kv_out = to_tokens(jnp.stack([key_grad, value_grad], axis=1))
    rows_out = kv_out.shape[0]
    key_out = kv_out[:, :, :, 0].reshape(rows_out, -1, depth)
    value_out = kv_out[:, :, :, 1].reshape(rows_out, -1, depth)
    return query_out, key_out, value_out


def solution(mesh):
    head, seq = mesh.devices.shape
    ring = WINDOW_LENGTH // BLOCK
    grouped = Mesh(mesh.devices.reshape(head, seq // ring, ring), ("head", "sh", "sl"))
    seq_axes = ("sh", "sl")
    placed = (
        P(seq_axes, "head", None),
        P(seq_axes, "head", None),
        P(seq_axes, "head", None),
        P(seq_axes, "head", None),
        P(seq_axes + ("head",), None, None),
        P("head", seq_axes),
        P(seq_axes),
    )
    out = P(seq_axes + ("head",), None, None)
    return jax.shard_map(
        on_device,
        mesh=grouped,
        in_specs=placed,
        out_specs=(out, out, out),
        check_vma=False,
    )
```

```python
from functools import partial

import jax
import jax.numpy as jnp
from jax import lax
from jax.experimental import pallas as pl
from jax.sharding import Mesh
from jax.sharding import PartitionSpec as P

WINDOW_LENGTH = 1024
BLOCK = 256

score_scale = 168.0 ** (-0.5)


def shifted(value, axis, by):
    size = lax.axis_size(axis)
    pairs = [(i, i + by) for i in range(size) if 0 <= i + by < size]
    return lax.ppermute(value, axis, pairs)


def band_terms(query, grad, logsum, delta, start, base, keys, values):
    group, tokens, depth = query.shape
    tiles = tokens // BLOCK
    span = WINDOW_LENGTH + BLOCK
    query_t = query.reshape(group, tiles, BLOCK, depth)
    grad_t = grad.reshape(group, tiles, BLOCK, depth)
    logsum_t = logsum.reshape(group, tiles, BLOCK).transpose(1, 0, 2)
    delta_t = delta.reshape(group, tiles, BLOCK).transpose(1, 0, 2)
    start_t = start.reshape(tiles, BLOCK)
    key_w = jnp.stack([keys[t * BLOCK : t * BLOCK + span] for t in range(tiles)])
    value_w = jnp.stack([values[t * BLOCK : t * BLOCK + span] for t in range(tiles)])
    tile_base = base + BLOCK * jnp.arange(tiles, dtype=jnp.int32)
    query_place = tile_base[:, None] + jnp.arange(BLOCK, dtype=jnp.int32)[None, :]
    key_place = tile_base[:, None] - WINDOW_LENGTH + jnp.arange(span, dtype=jnp.int32)[None, :]
    gap = query_place[:, :, None] - key_place[:, None, :]
    visible = (gap >= 0) & (gap < WINDOW_LENGTH) & (key_place[:, None, :] >= start_t[:, :, None])
    scores = (
        jnp.einsum("gtid,tjd->tgij", query_t, key_w, preferred_element_type=jnp.float32)
        * score_scale
    )
    probs = jnp.where(visible[:, None], jnp.exp(scores - logsum_t[..., None]), 0.0)
    dprobs = jnp.einsum("gtid,tjd->tgij", grad_t, value_w, preferred_element_type=jnp.float32)
    low_scores = (probs * (dprobs - delta_t[..., None])).astype(jnp.bfloat16)
    low_probs = probs.astype(jnp.bfloat16)
    query_term = jnp.einsum("tgij,tjd->tigd", low_scores, key_w, preferred_element_type=jnp.float32)
    key_w_term = jnp.einsum("tgij,gtid->tjd", low_scores, query_t, preferred_element_type=jnp.float32)
    value_w_term = jnp.einsum("tgij,gtid->tjd", low_probs, grad_t, preferred_element_type=jnp.float32)
    total = WINDOW_LENGTH + tokens
    key_term = jnp.zeros((total, depth), jnp.float32)
    value_term = jnp.zeros((total, depth), jnp.float32)
    for t in range(tiles):
        key_term = key_term.at[t * BLOCK : t * BLOCK + span].add(key_w_term[t])
        value_term = value_term.at[t * BLOCK : t * BLOCK + span].add(value_w_term[t])
    return query_term.reshape(tokens, group, depth), key_term, value_term


def band_kernel(halo, q_ref, g_ref, lse_ref, dl_ref, ps_ref, k_ref, v_ref, dq_ref, dk_ref, dv_ref):
    heads, tokens, depth = q_ref.shape
    tiles = tokens // BLOCK
    reach = WINDOW_LENGTH // BLOCK
    dk_ref[...] = jnp.zeros(dk_ref.shape, jnp.float32)
    dv_ref[...] = jnp.zeros(dv_ref.shape, jnp.float32)
    last = (((0,), (0,)), ((), ()))
    cross = (((1,), (1,)), ((), ()))
    gap = lax.broadcasted_iota(jnp.int32, (BLOCK, BLOCK), 0) - lax.broadcasted_iota(
        jnp.int32, (BLOCK, BLOCK), 1
    )
    col = lax.broadcasted_iota(jnp.int32, (BLOCK, BLOCK), 1)
    for t in range(tiles):
        rows = slice(t * BLOCK, (t + 1) * BLOCK)
        if halo:
            blocks = [(b, t + b) for b in range(reach - t)]
        else:
            blocks = [(b, t + b - reach) for b in range(reach - t, reach + 1)]
        starts = ps_ref[rows, :]
        for h in range(heads):
            query = q_ref[h, rows, :]
            grad = g_ref[h, rows, :]
            logsum = lse_ref[h, rows, :]
            delta = dl_ref[h, rows, :]
            query_acc = jnp.zeros((BLOCK, depth), jnp.float32)
            for b, kb in blocks:
                keys_at = slice(kb * BLOCK, (kb + 1) * BLOCK)
                key = k_ref[keys_at, :]
                value = v_ref[keys_at, :]
                scores = (
                    lax.dot_general(query, key, cross, preferred_element_type=jnp.float32)
                    * score_scale
                )
                key_first = kb * BLOCK + (0 if halo else WINDOW_LENGTH)
                visible = col >= starts - key_first
                if b == 0:
                    visible = visible & (gap < 0)
                if b == reach:
                    visible = visible & (gap >= 0)
                probs = jnp.where(visible, jnp.exp(scores - logsum), 0.0)
                dprobs = lax.dot_general(grad, value, cross, preferred_element_type=jnp.float32)
                low_scores = (probs * (dprobs - delta)).astype(jnp.bfloat16)
                query_acc = query_acc + jnp.dot(
                    low_scores, key, preferred_element_type=jnp.float32
                )
                dk_ref[keys_at, :] += lax.dot_general(
                    low_scores, query, last, preferred_element_type=jnp.float32
                )
                dv_ref[keys_at, :] += lax.dot_general(
                    probs.astype(jnp.bfloat16), grad, last, preferred_element_type=jnp.float32
                )
            dq_ref[h, rows, :] = query_acc


def band_part(halo, query, grad, logsum, delta, start_rel, keys, values):
    group, tokens, depth = query.shape
    total = keys.shape[0]
    return pl.pallas_call(
        partial(band_kernel, halo),
        out_shape=(
            jax.ShapeDtypeStruct((group, tokens, depth), jnp.float32),
            jax.ShapeDtypeStruct((total, depth), jnp.float32),
            jax.ShapeDtypeStruct((total, depth), jnp.float32),
        ),
    )(query, grad, logsum[..., None], delta[..., None], start_rel, keys, values)


def split_three(x):
    hi = lax.reduce_precision(x, exponent_bits=8, mantissa_bits=7)
    rest = x - hi
    mid = lax.reduce_precision(rest, exponent_bits=8, mantissa_bits=7)
    lo = rest - mid
    return jnp.stack([hi, mid, lo], axis=-1).astype(jnp.bfloat16)


def join_three(parts):
    parts = parts.astype(jnp.float32)
    return (parts[..., 0] + parts[..., 1]) + parts[..., 2]


def on_device(
    queries, normed_keys, value_matrix, forward_out, output_gradient, row_log_total, pair_start
):
    ring = lax.axis_size("sl")
    head_size = lax.axis_size("head")
    local_tokens, heads_local, depth = queries.shape
    kv_local = normed_keys.shape[1]
    heads_here = heads_local // ring
    kv_here = kv_local // ring
    grad_rows = output_gradient.shape[0]
    grad_g = output_gradient.reshape(grad_rows, head_size, ring, heads_here, depth)
    grad_g = grad_g.transpose(2, 1, 3, 0, 4).reshape(ring * head_size, heads_here, grad_rows, depth)
    logsum = row_log_total.reshape(ring, heads_here, local_tokens).transpose(0, 2, 1)
    side = jnp.concatenate(
        [
            split_three(logsum).reshape(ring, local_tokens, heads_here * 3),
            jnp.broadcast_to(
                split_three(pair_start.astype(jnp.float32))[None], (ring, local_tokens, 3)
            ),
        ],
        axis=2,
    )
    side = jnp.pad(side, ((0, 0), (0, 0), (0, depth - side.shape[2])))
    kv_packed = jnp.concatenate(
        [
            normed_keys.reshape(local_tokens, ring * kv_here, depth).transpose(1, 0, 2)[:, None],
            value_matrix.reshape(local_tokens, ring * kv_here, depth).transpose(1, 0, 2)[:, None],
            side[:, None],
        ],
        axis=1,
    )
    kv_packed = lax.all_to_all(kv_packed, "sl", split_axis=0, concat_axis=2, tiled=True)[0]
    far = shifted(kv_packed[:2], "sh", 1)
    grad_g, kv_packed = lax.optimization_barrier((grad_g, kv_packed))
    grad_g = lax.all_to_all(grad_g, ("sl", "head"), split_axis=0, concat_axis=2, tiled=True)[0]
    key_own = kv_packed[0]
    value_own = kv_packed[1]
    side_g = kv_packed[2]
    tokens = key_own.shape[0]
    logsum_g = join_three(side_g[:, : 3 * heads_here].reshape(tokens, heads_here, 3)).T
    start_g = jnp.round(join_three(side_g[:, 3 * heads_here : 3 * heads_here + 3])).astype(
        jnp.int32
    )
    qf_packed = jnp.concatenate(
        [
            queries.reshape(local_tokens, ring, heads_here, depth).transpose(1, 2, 0, 3),
            forward_out.reshape(local_tokens, ring, heads_here, depth).transpose(1, 2, 0, 3),
        ],
        axis=1,
    )
    qf_packed = lax.all_to_all(qf_packed, "sl", split_axis=0, concat_axis=2, tiled=True)[0]
    query_g = qf_packed[:heads_here]
    forward_g = qf_packed[heads_here:]
    delta_g = jnp.einsum("gtd,gtd->gt", forward_g, grad_g, preferred_element_type=jnp.float32)
    base = lax.axis_index("sh") * tokens
    start_rel = (start_g - base + WINDOW_LENGTH)[:, None]
    query_far, key_far, value_far = band_part(
        True, query_g, grad_g, logsum_g, delta_g, start_rel, far[0], far[1]
    )
    back = shifted(jnp.stack([key_far, value_far]).astype(jnp.bfloat16), "sh", -1)
    query_g, key_far = lax.optimization_barrier((query_g, key_far))
    query_own, key_sum, value_sum = band_part(
        False, query_g, grad_g, logsum_g, delta_g, start_rel, key_own, value_own
    )
    query_sum = (query_far + query_own).transpose(1, 0, 2)

    def to_tokens(x):
        items = x.shape[1]
        x = lax.all_to_all(x, ("sl", "head"), split_axis=0, concat_axis=1, tiled=True)
        rows_out = x.shape[0]
        return x.reshape(rows_out, ring, head_size, items, depth).transpose(0, 2, 1, 3, 4)

    key_total = key_sum + back[0].astype(jnp.float32)
    value_total = value_sum + back[1].astype(jnp.float32)
    query_grad = (query_sum * score_scale).astype(jnp.bfloat16)
    key_grad = (key_total * score_scale).astype(jnp.bfloat16)[:, None]
    value_grad = value_total.astype(jnp.bfloat16)[:, None]
    outs = to_tokens(jnp.concatenate([query_grad, key_grad, value_grad], axis=1))
    rows_out = outs.shape[0]
    query_out = outs[:, :, :, :heads_here].reshape(rows_out, -1, depth)
    key_out = outs[:, :, :, heads_here].reshape(rows_out, -1, depth)
    value_out = outs[:, :, :, heads_here + 1].reshape(rows_out, -1, depth)
    return query_out, key_out, value_out


def solution(mesh):
    head, seq = mesh.devices.shape
    ring = WINDOW_LENGTH // BLOCK
    grouped = Mesh(mesh.devices.reshape(head, seq // ring, ring), ("head", "sh", "sl"))
    seq_axes = ("sh", "sl")
    placed = (
        P(seq_axes, "head", None),
        P(seq_axes, "head", None),
        P(seq_axes, "head", None),
        P(seq_axes, "head", None),
        P(seq_axes + ("head",), None, None),
        P("head", seq_axes),
        P(seq_axes),
    )
    out = P(seq_axes + ("head",), None, None)
    return jax.shard_map(
        on_device,
        mesh=grouped,
        in_specs=placed,
        out_specs=(out, out, out),
        check_vma=False,
    )
```

```python
from functools import partial

import jax
import jax.numpy as jnp
from jax import lax
from jax.experimental import pallas as pl
from jax.sharding import Mesh
from jax.sharding import PartitionSpec as P

WINDOW_LENGTH = 1024
BLOCK = 256

score_scale = 168.0 ** (-0.5)


def shifted(value, axis, by):
    size = lax.axis_size(axis)
    pairs = [(i, i + by) for i in range(size) if 0 <= i + by < size]
    return lax.ppermute(value, axis, pairs)


def band_terms(query, grad, logsum, delta, start, base, keys, values):
    group, tokens, depth = query.shape
    tiles = tokens // BLOCK
    span = WINDOW_LENGTH + BLOCK
    query_t = query.reshape(group, tiles, BLOCK, depth)
    grad_t = grad.reshape(group, tiles, BLOCK, depth)
    logsum_t = logsum.reshape(group, tiles, BLOCK).transpose(1, 0, 2)
    delta_t = delta.reshape(group, tiles, BLOCK).transpose(1, 0, 2)
    start_t = start.reshape(tiles, BLOCK)
    key_w = jnp.stack([keys[t * BLOCK : t * BLOCK + span] for t in range(tiles)])
    value_w = jnp.stack([values[t * BLOCK : t * BLOCK + span] for t in range(tiles)])
    tile_base = base + BLOCK * jnp.arange(tiles, dtype=jnp.int32)
    query_place = tile_base[:, None] + jnp.arange(BLOCK, dtype=jnp.int32)[None, :]
    key_place = tile_base[:, None] - WINDOW_LENGTH + jnp.arange(span, dtype=jnp.int32)[None, :]
    gap = query_place[:, :, None] - key_place[:, None, :]
    visible = (gap >= 0) & (gap < WINDOW_LENGTH) & (key_place[:, None, :] >= start_t[:, :, None])
    scores = (
        jnp.einsum("gtid,tjd->tgij", query_t, key_w, preferred_element_type=jnp.float32)
        * score_scale
    )
    probs = jnp.where(visible[:, None], jnp.exp(scores - logsum_t[..., None]), 0.0)
    dprobs = jnp.einsum("gtid,tjd->tgij", grad_t, value_w, preferred_element_type=jnp.float32)
    low_scores = (probs * (dprobs - delta_t[..., None])).astype(jnp.bfloat16)
    low_probs = probs.astype(jnp.bfloat16)
    query_term = jnp.einsum("tgij,tjd->tigd", low_scores, key_w, preferred_element_type=jnp.float32)
    key_w_term = jnp.einsum("tgij,gtid->tjd", low_scores, query_t, preferred_element_type=jnp.float32)
    value_w_term = jnp.einsum("tgij,gtid->tjd", low_probs, grad_t, preferred_element_type=jnp.float32)
    total = WINDOW_LENGTH + tokens
    key_term = jnp.zeros((total, depth), jnp.float32)
    value_term = jnp.zeros((total, depth), jnp.float32)
    for t in range(tiles):
        key_term = key_term.at[t * BLOCK : t * BLOCK + span].add(key_w_term[t])
        value_term = value_term.at[t * BLOCK : t * BLOCK + span].add(value_w_term[t])
    return query_term.reshape(tokens, group, depth), key_term, value_term


def band_kernel(halo, q_ref, g_ref, lse_ref, dl_ref, ps_ref, k_ref, v_ref, dq_ref, dk_ref, dv_ref):
    heads, tokens, depth = q_ref.shape
    tiles = tokens // BLOCK
    reach = WINDOW_LENGTH // BLOCK
    dk_ref[...] = jnp.zeros(dk_ref.shape, jnp.float32)
    dv_ref[...] = jnp.zeros(dv_ref.shape, jnp.float32)
    first = (((0,), (0,)), ((), ()))
    cross = (((1,), (1,)), ((), ()))
    key_row = lax.broadcasted_iota(jnp.int32, (BLOCK, BLOCK), 0)
    gap = lax.broadcasted_iota(jnp.int32, (BLOCK, BLOCK), 1) - key_row
    for t in range(tiles):
        rows = slice(t * BLOCK, (t + 1) * BLOCK)
        if halo:
            blocks = [(b, t + b) for b in range(reach - t)]
        else:
            blocks = [(b, t + b - reach) for b in range(reach - t, reach + 1)]
        starts = ps_ref[:, rows]
        for h in range(heads):
            query = q_ref[h, rows, :]
            grad = g_ref[h, rows, :]
            logsum = lse_ref[h : h + 1, rows]
            delta = dl_ref[h : h + 1, rows]
            query_acc = jnp.zeros((BLOCK, depth), jnp.float32)
            for b, kb in blocks:
                keys_at = slice(kb * BLOCK, (kb + 1) * BLOCK)
                key = k_ref[keys_at, :]
                value = v_ref[keys_at, :]
                scores = (
                    lax.dot_general(key, query, cross, preferred_element_type=jnp.float32)
                    * score_scale
                )
                key_first = kb * BLOCK + (0 if halo else WINDOW_LENGTH)
                visible = key_row >= starts - key_first
                if b == 0:
                    visible = visible & (gap < 0)
                if b == reach:
                    visible = visible & (gap >= 0)
                probs = jnp.where(visible, jnp.exp(scores - logsum), 0.0)
                dprobs = lax.dot_general(value, grad, cross, preferred_element_type=jnp.float32)
                low_scores = (probs * (dprobs - delta)).astype(jnp.bfloat16)
                query_acc = query_acc + lax.dot_general(
                    low_scores, key, first, preferred_element_type=jnp.float32
                )
                dk_ref[keys_at, :] += jnp.dot(low_scores, query, preferred_element_type=jnp.float32)
                dv_ref[keys_at, :] += jnp.dot(
                    probs.astype(jnp.bfloat16), grad, preferred_element_type=jnp.float32
                )
            dq_ref[h, rows, :] = query_acc


def band_part(halo, query, grad, logsum, delta, start_rel, keys, values):
    group, tokens, depth = query.shape
    total = keys.shape[0]
    return pl.pallas_call(
        partial(band_kernel, halo),
        out_shape=(
            jax.ShapeDtypeStruct((group, tokens, depth), jnp.float32),
            jax.ShapeDtypeStruct((total, depth), jnp.float32),
            jax.ShapeDtypeStruct((total, depth), jnp.float32),
        ),
    )(query, grad, logsum, delta, start_rel, keys, values)


def split_three(x):
    hi = lax.reduce_precision(x, exponent_bits=8, mantissa_bits=7)
    rest = x - hi
    mid = lax.reduce_precision(rest, exponent_bits=8, mantissa_bits=7)
    lo = rest - mid
    return jnp.stack([hi, mid, lo], axis=-1).astype(jnp.bfloat16)


def join_three(parts):
    parts = parts.astype(jnp.float32)
    return (parts[..., 0] + parts[..., 1]) + parts[..., 2]


def on_device(
    queries, normed_keys, value_matrix, forward_out, output_gradient, row_log_total, pair_start
):
    ring = lax.axis_size("sl")
    head_size = lax.axis_size("head")
    local_tokens, heads_local, depth = queries.shape
    kv_local = normed_keys.shape[1]
    heads_here = heads_local // ring
    kv_here = kv_local // ring
    grad_rows = output_gradient.shape[0]
    grad_g = output_gradient.reshape(grad_rows, head_size, ring, heads_here, depth)
    grad_g = grad_g.transpose(2, 1, 3, 0, 4).reshape(ring * head_size, heads_here, grad_rows, depth)
    logsum = row_log_total.reshape(ring, heads_here, local_tokens).transpose(0, 2, 1)
    side = jnp.concatenate(
        [
            split_three(logsum).reshape(ring, local_tokens, heads_here * 3),
            jnp.broadcast_to(
                split_three(pair_start.astype(jnp.float32))[None], (ring, local_tokens, 3)
            ),
        ],
        axis=2,
    )
    side = jnp.pad(side, ((0, 0), (0, 0), (0, depth - side.shape[2])))
    kv_packed = jnp.concatenate(
        [
            normed_keys.reshape(local_tokens, ring * kv_here, depth).transpose(1, 0, 2)[:, None],
            value_matrix.reshape(local_tokens, ring * kv_here, depth).transpose(1, 0, 2)[:, None],
            side[:, None],
        ],
        axis=1,
    )
    kv_packed = lax.all_to_all(kv_packed, "sl", split_axis=0, concat_axis=2, tiled=True)[0]
    far = shifted(kv_packed[:2], "sh", 1)
    grad_g, kv_packed = lax.optimization_barrier((grad_g, kv_packed))
    grad_g = lax.all_to_all(grad_g, ("sl", "head"), split_axis=0, concat_axis=2, tiled=True)[0]
    key_own = kv_packed[0]
    value_own = kv_packed[1]
    side_g = kv_packed[2]
    tokens = key_own.shape[0]
    logsum_g = join_three(side_g[:, : 3 * heads_here].reshape(tokens, heads_here, 3)).T
    start_g = jnp.round(join_three(side_g[:, 3 * heads_here : 3 * heads_here + 3])).astype(
        jnp.int32
    )
    qf_packed = jnp.concatenate(
        [
            queries.reshape(local_tokens, ring, heads_here, depth).transpose(1, 2, 0, 3),
            forward_out.reshape(local_tokens, ring, heads_here, depth).transpose(1, 2, 0, 3),
        ],
        axis=1,
    )
    qf_packed = lax.all_to_all(qf_packed, "sl", split_axis=0, concat_axis=2, tiled=True)[0]
    query_g = qf_packed[:heads_here]
    forward_g = qf_packed[heads_here:]
    delta_g = jnp.einsum("gtd,gtd->gt", forward_g, grad_g, preferred_element_type=jnp.float32)
    base = lax.axis_index("sh") * tokens
    start_rel = (start_g - base + WINDOW_LENGTH)[None, :]
    query_far, key_far, value_far = band_part(
        True, query_g, grad_g, logsum_g, delta_g, start_rel, far[0], far[1]
    )
    back = shifted(jnp.stack([key_far, value_far]).astype(jnp.bfloat16), "sh", -1)
    query_g, key_far = lax.optimization_barrier((query_g, key_far))
    query_own, key_sum, value_sum = band_part(
        False, query_g, grad_g, logsum_g, delta_g, start_rel, key_own, value_own
    )
    query_sum = (query_far + query_own).transpose(1, 0, 2)

    def to_tokens(x):
        items = x.shape[1]
        x = lax.all_to_all(x, ("sl", "head"), split_axis=0, concat_axis=1, tiled=True)
        rows_out = x.shape[0]
        return x.reshape(rows_out, ring, head_size, items, depth).transpose(0, 2, 1, 3, 4)

    key_total = key_sum + back[0].astype(jnp.float32)
    value_total = value_sum + back[1].astype(jnp.float32)
    query_grad = (query_sum * score_scale).astype(jnp.bfloat16)
    key_grad = (key_total * score_scale).astype(jnp.bfloat16)[:, None]
    value_grad = value_total.astype(jnp.bfloat16)[:, None]
    outs = to_tokens(jnp.concatenate([query_grad, key_grad, value_grad], axis=1))
    rows_out = outs.shape[0]
    query_out = outs[:, :, :, :heads_here].reshape(rows_out, -1, depth)
    key_out = outs[:, :, :, heads_here].reshape(rows_out, -1, depth)
    value_out = outs[:, :, :, heads_here + 1].reshape(rows_out, -1, depth)
    return query_out, key_out, value_out


def solution(mesh):
    head, seq = mesh.devices.shape
    ring = WINDOW_LENGTH // BLOCK
    grouped = Mesh(mesh.devices.reshape(head, seq // ring, ring), ("head", "sh", "sl"))
    seq_axes = ("sh", "sl")
    placed = (
        P(seq_axes, "head", None),
        P(seq_axes, "head", None),
        P(seq_axes, "head", None),
        P(seq_axes, "head", None),
        P(seq_axes + ("head",), None, None),
        P("head", seq_axes),
        P(seq_axes),
    )
    out = P(seq_axes + ("head",), None, None)
    return jax.shard_map(
        on_device,
        mesh=grouped,
        in_specs=placed,
        out_specs=(out, out, out),
        check_vma=False,
    )
```

```python
from functools import partial

import jax
import jax.numpy as jnp
from jax import lax
from jax.experimental import pallas as pl
from jax.sharding import Mesh
from jax.sharding import PartitionSpec as P

WINDOW_LENGTH = 1024
BLOCK = 256

score_scale = 168.0 ** (-0.5)


def shifted(value, axis, by):
    size = lax.axis_size(axis)
    pairs = [(i, i + by) for i in range(size) if 0 <= i + by < size]
    return lax.ppermute(value, axis, pairs)


def band_terms(query, grad, logsum, delta, start, base, keys, values):
    group, tokens, depth = query.shape
    tiles = tokens // BLOCK
    span = WINDOW_LENGTH + BLOCK
    query_t = query.reshape(group, tiles, BLOCK, depth)
    grad_t = grad.reshape(group, tiles, BLOCK, depth)
    logsum_t = logsum.reshape(group, tiles, BLOCK).transpose(1, 0, 2)
    delta_t = delta.reshape(group, tiles, BLOCK).transpose(1, 0, 2)
    start_t = start.reshape(tiles, BLOCK)
    key_w = jnp.stack([keys[t * BLOCK : t * BLOCK + span] for t in range(tiles)])
    value_w = jnp.stack([values[t * BLOCK : t * BLOCK + span] for t in range(tiles)])
    tile_base = base + BLOCK * jnp.arange(tiles, dtype=jnp.int32)
    query_place = tile_base[:, None] + jnp.arange(BLOCK, dtype=jnp.int32)[None, :]
    key_place = tile_base[:, None] - WINDOW_LENGTH + jnp.arange(span, dtype=jnp.int32)[None, :]
    gap = query_place[:, :, None] - key_place[:, None, :]
    visible = (gap >= 0) & (gap < WINDOW_LENGTH) & (key_place[:, None, :] >= start_t[:, :, None])
    scores = (
        jnp.einsum("gtid,tjd->tgij", query_t, key_w, preferred_element_type=jnp.float32)
        * score_scale
    )
    probs = jnp.where(visible[:, None], jnp.exp(scores - logsum_t[..., None]), 0.0)
    dprobs = jnp.einsum("gtid,tjd->tgij", grad_t, value_w, preferred_element_type=jnp.float32)
    low_scores = (probs * (dprobs - delta_t[..., None])).astype(jnp.bfloat16)
    low_probs = probs.astype(jnp.bfloat16)
    query_term = jnp.einsum("tgij,tjd->tigd", low_scores, key_w, preferred_element_type=jnp.float32)
    key_w_term = jnp.einsum("tgij,gtid->tjd", low_scores, query_t, preferred_element_type=jnp.float32)
    value_w_term = jnp.einsum("tgij,gtid->tjd", low_probs, grad_t, preferred_element_type=jnp.float32)
    total = WINDOW_LENGTH + tokens
    key_term = jnp.zeros((total, depth), jnp.float32)
    value_term = jnp.zeros((total, depth), jnp.float32)
    for t in range(tiles):
        key_term = key_term.at[t * BLOCK : t * BLOCK + span].add(key_w_term[t])
        value_term = value_term.at[t * BLOCK : t * BLOCK + span].add(value_w_term[t])
    return query_term.reshape(tokens, group, depth), key_term, value_term


def band_kernel(halo, q_ref, g_ref, lse_ref, dl_ref, ps_ref, k_ref, v_ref, dq_ref, dk_ref, dv_ref):
    heads, tokens, depth = q_ref.shape
    tiles = tokens // BLOCK
    reach = WINDOW_LENGTH // BLOCK
    dk_ref[...] = jnp.zeros(dk_ref.shape, jnp.float32)
    dv_ref[...] = jnp.zeros(dv_ref.shape, jnp.float32)
    first = (((0,), (0,)), ((), ()))
    cross = (((1,), (1,)), ((), ()))
    width = heads * BLOCK
    key_row = lax.broadcasted_iota(jnp.int32, (BLOCK, width), 0)
    gap = lax.broadcasted_iota(jnp.int32, (BLOCK, width), 1) % BLOCK - key_row
    for t in range(tiles):
        rows = slice(t * BLOCK, (t + 1) * BLOCK)
        if halo:
            blocks = [(b, t + b) for b in range(reach - t)]
        else:
            blocks = [(b, t + b - reach) for b in range(reach - t, reach + 1)]
        starts = jnp.concatenate([ps_ref[:, rows]] * heads, axis=1)
        query = jnp.concatenate([q_ref[h, rows, :] for h in range(heads)], axis=0)
        grad = jnp.concatenate([g_ref[h, rows, :] for h in range(heads)], axis=0)
        logsum = jnp.concatenate([lse_ref[h : h + 1, rows] for h in range(heads)], axis=1)
        delta = jnp.concatenate([dl_ref[h : h + 1, rows] for h in range(heads)], axis=1)
        query_acc = jnp.zeros((width, depth), jnp.float32)
        for b, kb in blocks:
            keys_at = slice(kb * BLOCK, (kb + 1) * BLOCK)
            key = k_ref[keys_at, :]
            value = v_ref[keys_at, :]
            scores = (
                lax.dot_general(key, query, cross, preferred_element_type=jnp.float32)
                * score_scale
            )
            key_first = kb * BLOCK + (0 if halo else WINDOW_LENGTH)
            visible = key_row >= starts - key_first
            if b == 0:
                visible = visible & (gap < 0)
            if b == reach:
                visible = visible & (gap >= 0)
            probs = jnp.where(visible, jnp.exp(scores - logsum), 0.0)
            dprobs = lax.dot_general(value, grad, cross, preferred_element_type=jnp.float32)
            low_scores = (probs * (dprobs - delta)).astype(jnp.bfloat16)
            query_acc = query_acc + lax.dot_general(
                low_scores, key, first, preferred_element_type=jnp.float32
            )
            dk_ref[keys_at, :] += jnp.dot(low_scores, query, preferred_element_type=jnp.float32)
            dv_ref[keys_at, :] += jnp.dot(
                probs.astype(jnp.bfloat16), grad, preferred_element_type=jnp.float32
            )
        for h in range(heads):
            dq_ref[h, rows, :] = query_acc[h * BLOCK : (h + 1) * BLOCK]


def band_part(halo, query, grad, logsum, delta, start_rel, keys, values):
    group, tokens, depth = query.shape
    total = keys.shape[0]
    return pl.pallas_call(
        partial(band_kernel, halo),
        out_shape=(
            jax.ShapeDtypeStruct((group, tokens, depth), jnp.float32),
            jax.ShapeDtypeStruct((total, depth), jnp.float32),
            jax.ShapeDtypeStruct((total, depth), jnp.float32),
        ),
    )(query, grad, logsum, delta, start_rel, keys, values)


def split_three(x):
    hi = lax.reduce_precision(x, exponent_bits=8, mantissa_bits=7)
    rest = x - hi
    mid = lax.reduce_precision(rest, exponent_bits=8, mantissa_bits=7)
    lo = rest - mid
    return jnp.stack([hi, mid, lo], axis=-1).astype(jnp.bfloat16)


def join_three(parts):
    parts = parts.astype(jnp.float32)
    return (parts[..., 0] + parts[..., 1]) + parts[..., 2]


def on_device(
    queries, normed_keys, value_matrix, forward_out, output_gradient, row_log_total, pair_start
):
    ring = lax.axis_size("sl")
    head_size = lax.axis_size("head")
    local_tokens, heads_local, depth = queries.shape
    kv_local = normed_keys.shape[1]
    heads_here = heads_local // ring
    kv_here = kv_local // ring
    grad_rows = output_gradient.shape[0]
    grad_g = output_gradient.reshape(grad_rows, head_size, ring, heads_here, depth)
    grad_g = grad_g.transpose(2, 1, 3, 0, 4).reshape(ring * head_size, heads_here, grad_rows, depth)
    logsum = row_log_total.reshape(ring, heads_here, local_tokens).transpose(0, 2, 1)
    side = jnp.concatenate(
        [
            split_three(logsum).reshape(ring, local_tokens, heads_here * 3),
            jnp.broadcast_to(
                split_three(pair_start.astype(jnp.float32))[None], (ring, local_tokens, 3)
            ),
        ],
        axis=2,
    )
    side = jnp.pad(side, ((0, 0), (0, 0), (0, depth - side.shape[2])))
    kv_packed = jnp.concatenate(
        [
            normed_keys.reshape(local_tokens, ring * kv_here, depth).transpose(1, 0, 2)[:, None],
            value_matrix.reshape(local_tokens, ring * kv_here, depth).transpose(1, 0, 2)[:, None],
            side[:, None],
        ],
        axis=1,
    )
    kv_packed = lax.all_to_all(kv_packed, "sl", split_axis=0, concat_axis=2, tiled=True)[0]
    far = shifted(kv_packed[:2], "sh", 1)
    grad_g, kv_packed = lax.optimization_barrier((grad_g, kv_packed))
    grad_g = lax.all_to_all(grad_g, ("sl", "head"), split_axis=0, concat_axis=2, tiled=True)[0]
    key_own = kv_packed[0]
    value_own = kv_packed[1]
    side_g = kv_packed[2]
    tokens = key_own.shape[0]
    logsum_g = join_three(side_g[:, : 3 * heads_here].reshape(tokens, heads_here, 3)).T
    start_g = jnp.round(join_three(side_g[:, 3 * heads_here : 3 * heads_here + 3])).astype(
        jnp.int32
    )
    qf_packed = jnp.concatenate(
        [
            queries.reshape(local_tokens, ring, heads_here, depth).transpose(1, 2, 0, 3),
            forward_out.reshape(local_tokens, ring, heads_here, depth).transpose(1, 2, 0, 3),
        ],
        axis=1,
    )
    qf_packed = lax.all_to_all(qf_packed, "sl", split_axis=0, concat_axis=2, tiled=True)[0]
    query_g = qf_packed[:heads_here]
    forward_g = qf_packed[heads_here:]
    delta_g = jnp.einsum("gtd,gtd->gt", forward_g, grad_g, preferred_element_type=jnp.float32)
    base = lax.axis_index("sh") * tokens
    start_rel = (start_g - base + WINDOW_LENGTH)[None, :]
    query_far, key_far, value_far = band_part(
        True, query_g, grad_g, logsum_g, delta_g, start_rel, far[0], far[1]
    )
    back = shifted(jnp.stack([key_far, value_far]).astype(jnp.bfloat16), "sh", -1)
    query_g, key_far = lax.optimization_barrier((query_g, key_far))
    query_own, key_sum, value_sum = band_part(
        False, query_g, grad_g, logsum_g, delta_g, start_rel, key_own, value_own
    )
    query_sum = (query_far + query_own).transpose(1, 0, 2)

    def to_tokens(x):
        items = x.shape[1]
        x = lax.all_to_all(x, ("sl", "head"), split_axis=0, concat_axis=1, tiled=True)
        rows_out = x.shape[0]
        return x.reshape(rows_out, ring, head_size, items, depth).transpose(0, 2, 1, 3, 4)

    key_total = key_sum + back[0].astype(jnp.float32)
    value_total = value_sum + back[1].astype(jnp.float32)
    query_grad = (query_sum * score_scale).astype(jnp.bfloat16)
    key_grad = (key_total * score_scale).astype(jnp.bfloat16)[:, None]
    value_grad = value_total.astype(jnp.bfloat16)[:, None]
    outs = to_tokens(jnp.concatenate([query_grad, key_grad, value_grad], axis=1))
    rows_out = outs.shape[0]
    query_out = outs[:, :, :, :heads_here].reshape(rows_out, -1, depth)
    key_out = outs[:, :, :, heads_here].reshape(rows_out, -1, depth)
    value_out = outs[:, :, :, heads_here + 1].reshape(rows_out, -1, depth)
    return query_out, key_out, value_out


def solution(mesh):
    head, seq = mesh.devices.shape
    ring = WINDOW_LENGTH // BLOCK
    grouped = Mesh(mesh.devices.reshape(head, seq // ring, ring), ("head", "sh", "sl"))
    seq_axes = ("sh", "sl")
    placed = (
        P(seq_axes, "head", None),
        P(seq_axes, "head", None),
        P(seq_axes, "head", None),
        P(seq_axes, "head", None),
        P(seq_axes + ("head",), None, None),
        P("head", seq_axes),
        P(seq_axes),
    )
    out = P(seq_axes + ("head",), None, None)
    return jax.shard_map(
        on_device,
        mesh=grouped,
        in_specs=placed,
        out_specs=(out, out, out),
        check_vma=False,
    )
```

```python
from functools import partial

import jax
import jax.numpy as jnp
from jax import lax
from jax.experimental import pallas as pl
from jax.experimental.pallas import tpu as pltpu
from jax.sharding import Mesh
from jax.sharding import PartitionSpec as P

WINDOW_LENGTH = 1024
BLOCK = 256

score_scale = 168.0 ** (-0.5)


def shifted(value, axis, by):
    size = lax.axis_size(axis)
    pairs = [(i, i + by) for i in range(size) if 0 <= i + by < size]
    return lax.ppermute(value, axis, pairs)


def band_terms(query, grad, logsum, delta, start, base, keys, values):
    group, tokens, depth = query.shape
    tiles = tokens // BLOCK
    span = WINDOW_LENGTH + BLOCK
    query_t = query.reshape(group, tiles, BLOCK, depth)
    grad_t = grad.reshape(group, tiles, BLOCK, depth)
    logsum_t = logsum.reshape(group, tiles, BLOCK).transpose(1, 0, 2)
    delta_t = delta.reshape(group, tiles, BLOCK).transpose(1, 0, 2)
    start_t = start.reshape(tiles, BLOCK)
    key_w = jnp.stack([keys[t * BLOCK : t * BLOCK + span] for t in range(tiles)])
    value_w = jnp.stack([values[t * BLOCK : t * BLOCK + span] for t in range(tiles)])
    tile_base = base + BLOCK * jnp.arange(tiles, dtype=jnp.int32)
    query_place = tile_base[:, None] + jnp.arange(BLOCK, dtype=jnp.int32)[None, :]
    key_place = tile_base[:, None] - WINDOW_LENGTH + jnp.arange(span, dtype=jnp.int32)[None, :]
    gap = query_place[:, :, None] - key_place[:, None, :]
    visible = (gap >= 0) & (gap < WINDOW_LENGTH) & (key_place[:, None, :] >= start_t[:, :, None])
    scores = (
        jnp.einsum("gtid,tjd->tgij", query_t, key_w, preferred_element_type=jnp.float32)
        * score_scale
    )
    probs = jnp.where(visible[:, None], jnp.exp(scores - logsum_t[..., None]), 0.0)
    dprobs = jnp.einsum("gtid,tjd->tgij", grad_t, value_w, preferred_element_type=jnp.float32)
    low_scores = (probs * (dprobs - delta_t[..., None])).astype(jnp.bfloat16)
    low_probs = probs.astype(jnp.bfloat16)
    query_term = jnp.einsum("tgij,tjd->tigd", low_scores, key_w, preferred_element_type=jnp.float32)
    key_w_term = jnp.einsum("tgij,gtid->tjd", low_scores, query_t, preferred_element_type=jnp.float32)
    value_w_term = jnp.einsum("tgij,gtid->tjd", low_probs, grad_t, preferred_element_type=jnp.float32)
    total = WINDOW_LENGTH + tokens
    key_term = jnp.zeros((total, depth), jnp.float32)
    value_term = jnp.zeros((total, depth), jnp.float32)
    for t in range(tiles):
        key_term = key_term.at[t * BLOCK : t * BLOCK + span].add(key_w_term[t])
        value_term = value_term.at[t * BLOCK : t * BLOCK + span].add(value_w_term[t])
    return query_term.reshape(tokens, group, depth), key_term, value_term


def band_kernel(halo, q_ref, g_ref, lse_ref, dl_ref, ps_ref, k_ref, v_ref, dq_ref, *rest):
    heads, tokens, depth = q_ref.shape
    tiles = tokens // BLOCK
    reach = WINDOW_LENGTH // BLOCK
    if halo:
        low_ref, dk_ref, dv_ref = rest
    else:
        dk_ref, dv_ref = rest
    dk_ref[...] = jnp.zeros(dk_ref.shape, jnp.float32)
    dv_ref[...] = jnp.zeros(dv_ref.shape, jnp.float32)
    first = (((0,), (0,)), ((), ()))
    cross = (((1,), (1,)), ((), ()))
    width = heads * BLOCK
    key_row = lax.broadcasted_iota(jnp.int32, (BLOCK, width), 0)
    gap = lax.broadcasted_iota(jnp.int32, (BLOCK, width), 1) % BLOCK - key_row
    for t in range(tiles):
        rows = slice(t * BLOCK, (t + 1) * BLOCK)
        if halo:
            blocks = [(b, t + b) for b in range(reach - t)]
        else:
            blocks = [(b, t + b - reach) for b in range(reach - t, reach + 1)]
        starts = jnp.concatenate([ps_ref[:, rows]] * heads, axis=1)
        query = jnp.concatenate([q_ref[h, rows, :] for h in range(heads)], axis=0)
        grad = jnp.concatenate([g_ref[h, rows, :] for h in range(heads)], axis=0)
        logsum = jnp.concatenate([lse_ref[h : h + 1, rows] for h in range(heads)], axis=1)
        delta = jnp.concatenate([dl_ref[h : h + 1, rows] for h in range(heads)], axis=1)
        query_acc = jnp.zeros((width, depth), jnp.float32)
        for b, kb in blocks:
            keys_at = slice(kb * BLOCK, (kb + 1) * BLOCK)
            key = k_ref[keys_at, :]
            value = v_ref[keys_at, :]
            scores = (
                lax.dot_general(key, query, cross, preferred_element_type=jnp.float32)
                * score_scale
            )
            key_first = kb * BLOCK + (0 if halo else WINDOW_LENGTH)
            visible = key_row >= starts - key_first
            if b == 0:
                visible = visible & (gap < 0)
            if b == reach:
                visible = visible & (gap >= 0)
            probs = jnp.where(visible, jnp.exp(scores - logsum), 0.0)
            dprobs = lax.dot_general(value, grad, cross, preferred_element_type=jnp.float32)
            low_scores = (probs * (dprobs - delta)).astype(jnp.bfloat16)
            query_acc = query_acc + lax.dot_general(
                low_scores, key, first, preferred_element_type=jnp.float32
            )
            dk_ref[keys_at, :] += jnp.dot(low_scores, query, preferred_element_type=jnp.float32)
            dv_ref[keys_at, :] += jnp.dot(
                probs.astype(jnp.bfloat16), grad, preferred_element_type=jnp.float32
            )
        for h in range(heads):
            dq_ref[h, rows, :] = query_acc[h * BLOCK : (h + 1) * BLOCK]
    if halo:
        low_ref[0] = dk_ref[...].astype(jnp.bfloat16)
        low_ref[1] = dv_ref[...].astype(jnp.bfloat16)


def band_part(halo, query, grad, logsum, delta, start_rel, keys, values):
    group, tokens, depth = query.shape
    total = keys.shape[0]
    sums = (
        jax.ShapeDtypeStruct((total, depth), jnp.float32),
        jax.ShapeDtypeStruct((total, depth), jnp.float32),
    )
    dq = jax.ShapeDtypeStruct((group, tokens, depth), jnp.float32)
    if halo:
        outs = (dq, jax.ShapeDtypeStruct((2, total, depth), jnp.bfloat16))
        scratch = [pltpu.VMEM((total, depth), jnp.float32)] * 2
    else:
        outs = (dq,) + sums
        scratch = []
    return pl.pallas_call(
        partial(band_kernel, halo), out_shape=outs, scratch_shapes=scratch
    )(query, grad, logsum, delta, start_rel, keys, values)


def split_three(x):
    hi = lax.reduce_precision(x, exponent_bits=8, mantissa_bits=7)
    rest = x - hi
    mid = lax.reduce_precision(rest, exponent_bits=8, mantissa_bits=7)
    lo = rest - mid
    return jnp.stack([hi, mid, lo], axis=-1).astype(jnp.bfloat16)


def join_three(parts):
    parts = parts.astype(jnp.float32)
    return (parts[..., 0] + parts[..., 1]) + parts[..., 2]


def on_device(
    queries, normed_keys, value_matrix, forward_out, output_gradient, row_log_total, pair_start
):
    ring = lax.axis_size("sl")
    head_size = lax.axis_size("head")
    local_tokens, heads_local, depth = queries.shape
    kv_local = normed_keys.shape[1]
    heads_here = heads_local // ring
    kv_here = kv_local // ring
    grad_rows = output_gradient.shape[0]
    grad_g = output_gradient.reshape(grad_rows, head_size, ring, heads_here, depth)
    grad_g = grad_g.transpose(2, 1, 3, 0, 4).reshape(ring * head_size, heads_here, grad_rows, depth)
    logsum = row_log_total.reshape(ring, heads_here, local_tokens).transpose(0, 2, 1)
    side = jnp.concatenate(
        [
            split_three(logsum).reshape(ring, local_tokens, heads_here * 3),
            jnp.broadcast_to(
                split_three(pair_start.astype(jnp.float32))[None], (ring, local_tokens, 3)
            ),
        ],
        axis=2,
    )
    side = jnp.pad(side, ((0, 0), (0, 0), (0, depth - side.shape[2])))
    kv_packed = jnp.concatenate(
        [
            normed_keys.reshape(local_tokens, ring * kv_here, depth).transpose(1, 0, 2)[:, None],
            value_matrix.reshape(local_tokens, ring * kv_here, depth).transpose(1, 0, 2)[:, None],
            side[:, None],
        ],
        axis=1,
    )
    kv_packed = lax.all_to_all(kv_packed, "sl", split_axis=0, concat_axis=2, tiled=True)[0]
    far = shifted(kv_packed[:2], "sh", 1)
    grad_g, kv_packed = lax.optimization_barrier((grad_g, kv_packed))
    grad_g = lax.all_to_all(grad_g, ("sl", "head"), split_axis=0, concat_axis=2, tiled=True)[0]
    key_own = kv_packed[0]
    value_own = kv_packed[1]
    side_g = kv_packed[2]
    tokens = key_own.shape[0]
    logsum_g = join_three(side_g[:, : 3 * heads_here].reshape(tokens, heads_here, 3)).T
    start_g = jnp.round(join_three(side_g[:, 3 * heads_here : 3 * heads_here + 3])).astype(
        jnp.int32
    )
    qf_packed = jnp.concatenate(
        [
            queries.reshape(local_tokens, ring, heads_here, depth).transpose(1, 2, 0, 3),
            forward_out.reshape(local_tokens, ring, heads_here, depth).transpose(1, 2, 0, 3),
        ],
        axis=1,
    )
    qf_packed = lax.all_to_all(qf_packed, "sl", split_axis=0, concat_axis=2, tiled=True)[0]
    query_g = qf_packed[:heads_here]
    forward_g = qf_packed[heads_here:]
    delta_g = jnp.einsum("gtd,gtd->gt", forward_g, grad_g, preferred_element_type=jnp.float32)
    base = lax.axis_index("sh") * tokens
    start_rel = (start_g - base + WINDOW_LENGTH)[None, :]
    query_far, key_far = band_part(
        True, query_g, grad_g, logsum_g, delta_g, start_rel, far[0], far[1]
    )
    back = shifted(key_far, "sh", -1)
    query_g, key_far = lax.optimization_barrier((query_g, key_far))
    query_own, key_sum, value_sum = band_part(
        False, query_g, grad_g, logsum_g, delta_g, start_rel, key_own, value_own
    )
    query_sum = (query_far + query_own).transpose(1, 0, 2)

    def to_tokens(x):
        items = x.shape[1]
        x = lax.all_to_all(x, ("sl", "head"), split_axis=0, concat_axis=1, tiled=True)
        rows_out = x.shape[0]
        return x.reshape(rows_out, ring, head_size, items, depth).transpose(0, 2, 1, 3, 4)

    key_total = key_sum + back[0].astype(jnp.float32)
    value_total = value_sum + back[1].astype(jnp.float32)
    query_grad = (query_sum * score_scale).astype(jnp.bfloat16)
    key_grad = (key_total * score_scale).astype(jnp.bfloat16)[:, None]
    value_grad = value_total.astype(jnp.bfloat16)[:, None]
    outs = to_tokens(jnp.concatenate([query_grad, key_grad, value_grad], axis=1))
    rows_out = outs.shape[0]
    query_out = outs[:, :, :, :heads_here].reshape(rows_out, -1, depth)
    key_out = outs[:, :, :, heads_here].reshape(rows_out, -1, depth)
    value_out = outs[:, :, :, heads_here + 1].reshape(rows_out, -1, depth)
    return query_out, key_out, value_out


def solution(mesh):
    head, seq = mesh.devices.shape
    ring = WINDOW_LENGTH // BLOCK
    grouped = Mesh(mesh.devices.reshape(head, seq // ring, ring), ("head", "sh", "sl"))
    seq_axes = ("sh", "sl")
    placed = (
        P(seq_axes, "head", None),
        P(seq_axes, "head", None),
        P(seq_axes, "head", None),
        P(seq_axes, "head", None),
        P(seq_axes + ("head",), None, None),
        P("head", seq_axes),
        P(seq_axes),
    )
    out = P(seq_axes + ("head",), None, None)
    return jax.shard_map(
        on_device,
        mesh=grouped,
        in_specs=placed,
        out_specs=(out, out, out),
        check_vma=False,
    )
```

```python
from functools import partial

import jax
import jax.numpy as jnp
from jax import lax
from jax.experimental import pallas as pl
from jax.experimental.pallas import tpu as pltpu
from jax.sharding import Mesh
from jax.sharding import PartitionSpec as P

WINDOW_LENGTH = 1024
BLOCK = 256

score_scale = 168.0 ** (-0.5)


def shifted(value, axis, by):
    size = lax.axis_size(axis)
    pairs = [(i, i + by) for i in range(size) if 0 <= i + by < size]
    return lax.ppermute(value, axis, pairs)


def band_terms(query, grad, logsum, delta, start, base, keys, values):
    group, tokens, depth = query.shape
    tiles = tokens // BLOCK
    span = WINDOW_LENGTH + BLOCK
    query_t = query.reshape(group, tiles, BLOCK, depth)
    grad_t = grad.reshape(group, tiles, BLOCK, depth)
    logsum_t = logsum.reshape(group, tiles, BLOCK).transpose(1, 0, 2)
    delta_t = delta.reshape(group, tiles, BLOCK).transpose(1, 0, 2)
    start_t = start.reshape(tiles, BLOCK)
    key_w = jnp.stack([keys[t * BLOCK : t * BLOCK + span] for t in range(tiles)])
    value_w = jnp.stack([values[t * BLOCK : t * BLOCK + span] for t in range(tiles)])
    tile_base = base + BLOCK * jnp.arange(tiles, dtype=jnp.int32)
    query_place = tile_base[:, None] + jnp.arange(BLOCK, dtype=jnp.int32)[None, :]
    key_place = tile_base[:, None] - WINDOW_LENGTH + jnp.arange(span, dtype=jnp.int32)[None, :]
    gap = query_place[:, :, None] - key_place[:, None, :]
    visible = (gap >= 0) & (gap < WINDOW_LENGTH) & (key_place[:, None, :] >= start_t[:, :, None])
    scores = (
        jnp.einsum("gtid,tjd->tgij", query_t, key_w, preferred_element_type=jnp.float32)
        * score_scale
    )
    probs = jnp.where(visible[:, None], jnp.exp(scores - logsum_t[..., None]), 0.0)
    dprobs = jnp.einsum("gtid,tjd->tgij", grad_t, value_w, preferred_element_type=jnp.float32)
    low_scores = (probs * (dprobs - delta_t[..., None])).astype(jnp.bfloat16)
    low_probs = probs.astype(jnp.bfloat16)
    query_term = jnp.einsum("tgij,tjd->tigd", low_scores, key_w, preferred_element_type=jnp.float32)
    key_w_term = jnp.einsum("tgij,gtid->tjd", low_scores, query_t, preferred_element_type=jnp.float32)
    value_w_term = jnp.einsum("tgij,gtid->tjd", low_probs, grad_t, preferred_element_type=jnp.float32)
    total = WINDOW_LENGTH + tokens
    key_term = jnp.zeros((total, depth), jnp.float32)
    value_term = jnp.zeros((total, depth), jnp.float32)
    for t in range(tiles):
        key_term = key_term.at[t * BLOCK : t * BLOCK + span].add(key_w_term[t])
        value_term = value_term.at[t * BLOCK : t * BLOCK + span].add(value_w_term[t])
    return query_term.reshape(tokens, group, depth), key_term, value_term


def band_kernel(halo, q_ref, g_ref, lse_ref, dl_ref, ps_ref, k_ref, v_ref, *rest):
    heads, tokens, depth = q_ref.shape
    tiles = tokens // BLOCK
    reach = WINDOW_LENGTH // BLOCK
    if halo:
        dq_ref, low_ref, dk_ref, dv_ref = rest
    else:
        dq_in_ref, dq_ref, dk_ref, dv_ref = rest
    dk_ref[...] = jnp.zeros(dk_ref.shape, jnp.float32)
    dv_ref[...] = jnp.zeros(dv_ref.shape, jnp.float32)
    first = (((0,), (0,)), ((), ()))
    cross = (((1,), (1,)), ((), ()))
    width = heads * BLOCK
    key_row = lax.broadcasted_iota(jnp.int32, (BLOCK, width), 0)
    gap = lax.broadcasted_iota(jnp.int32, (BLOCK, width), 1) % BLOCK - key_row
    for t in range(tiles):
        rows = slice(t * BLOCK, (t + 1) * BLOCK)
        if halo:
            blocks = [(b, t + b) for b in range(reach - t)]
        else:
            blocks = [(b, t + b - reach) for b in range(reach - t, reach + 1)]
        starts = jnp.concatenate([ps_ref[:, rows]] * heads, axis=1)
        query = jnp.concatenate([q_ref[h, rows, :] for h in range(heads)], axis=0)
        grad = jnp.concatenate([g_ref[h, rows, :] for h in range(heads)], axis=0)
        logsum = jnp.concatenate([lse_ref[h : h + 1, rows] for h in range(heads)], axis=1)
        delta = jnp.concatenate([dl_ref[h : h + 1, rows] for h in range(heads)], axis=1)
        if halo:
            query_acc = jnp.zeros((width, depth), jnp.float32)
        else:
            query_acc = jnp.concatenate([dq_in_ref[h, rows, :] for h in range(heads)], axis=0)
        for b, kb in blocks:
            keys_at = slice(kb * BLOCK, (kb + 1) * BLOCK)
            key = k_ref[keys_at, :]
            value = v_ref[keys_at, :]
            scores = (
                lax.dot_general(key, query, cross, preferred_element_type=jnp.float32)
                * score_scale
            )
            key_first = kb * BLOCK + (0 if halo else WINDOW_LENGTH)
            visible = key_row >= starts - key_first
            if b == 0:
                visible = visible & (gap < 0)
            if b == reach:
                visible = visible & (gap >= 0)
            probs = jnp.where(visible, jnp.exp(scores - logsum), 0.0)
            dprobs = lax.dot_general(value, grad, cross, preferred_element_type=jnp.float32)
            low_scores = (probs * (dprobs - delta)).astype(jnp.bfloat16)
            query_acc = query_acc + lax.dot_general(
                low_scores, key, first, preferred_element_type=jnp.float32
            )
            dk_ref[keys_at, :] += jnp.dot(low_scores, query, preferred_element_type=jnp.float32)
            dv_ref[keys_at, :] += jnp.dot(
                probs.astype(jnp.bfloat16), grad, preferred_element_type=jnp.float32
            )
        for h in range(heads):
            part = query_acc[h * BLOCK : (h + 1) * BLOCK]
            dq_ref[h, rows, :] = part if halo else (part * score_scale).astype(jnp.bfloat16)
    if halo:
        low_ref[0] = dk_ref[...].astype(jnp.bfloat16)
        low_ref[1] = dv_ref[...].astype(jnp.bfloat16)


def band_part(halo, query, grad, logsum, delta, start_rel, keys, values, dq_in=None):
    group, tokens, depth = query.shape
    total = keys.shape[0]
    sums = (
        jax.ShapeDtypeStruct((total, depth), jnp.float32),
        jax.ShapeDtypeStruct((total, depth), jnp.float32),
    )
    if halo:
        dq = jax.ShapeDtypeStruct((group, tokens, depth), jnp.float32)
        outs = (dq, jax.ShapeDtypeStruct((2, total, depth), jnp.bfloat16))
        scratch = [pltpu.VMEM((total, depth), jnp.float32)] * 2
        extra = ()
    else:
        dq = jax.ShapeDtypeStruct((group, tokens, depth), jnp.bfloat16)
        outs = (dq,) + sums
        scratch = []
        extra = (dq_in,)
    return pl.pallas_call(
        partial(band_kernel, halo), out_shape=outs, scratch_shapes=scratch
    )(query, grad, logsum, delta, start_rel, keys, values, *extra)


def split_three(x):
    hi = lax.reduce_precision(x, exponent_bits=8, mantissa_bits=7)
    rest = x - hi
    mid = lax.reduce_precision(rest, exponent_bits=8, mantissa_bits=7)
    lo = rest - mid
    return jnp.stack([hi, mid, lo], axis=-1).astype(jnp.bfloat16)


def join_three(parts):
    parts = parts.astype(jnp.float32)
    return (parts[..., 0] + parts[..., 1]) + parts[..., 2]


def on_device(
    queries, normed_keys, value_matrix, forward_out, output_gradient, row_log_total, pair_start
):
    ring = lax.axis_size("sl")
    head_size = lax.axis_size("head")
    local_tokens, heads_local, depth = queries.shape
    kv_local = normed_keys.shape[1]
    heads_here = heads_local // ring
    kv_here = kv_local // ring
    grad_rows = output_gradient.shape[0]
    grad_g = output_gradient.reshape(grad_rows, head_size, ring, heads_here, depth)
    grad_g = grad_g.transpose(2, 1, 3, 0, 4).reshape(ring * head_size, heads_here, grad_rows, depth)
    logsum = row_log_total.reshape(ring, heads_here, local_tokens).transpose(0, 2, 1)
    side = jnp.concatenate(
        [
            split_three(logsum).reshape(ring, local_tokens, heads_here * 3),
            jnp.broadcast_to(
                split_three(pair_start.astype(jnp.float32))[None], (ring, local_tokens, 3)
            ),
        ],
        axis=2,
    )
    side = jnp.pad(side, ((0, 0), (0, 0), (0, depth - side.shape[2])))
    kv_packed = jnp.concatenate(
        [
            normed_keys.reshape(local_tokens, ring * kv_here, depth).transpose(1, 0, 2)[:, None],
            value_matrix.reshape(local_tokens, ring * kv_here, depth).transpose(1, 0, 2)[:, None],
            side[:, None],
        ],
        axis=1,
    )
    kv_packed = lax.all_to_all(kv_packed, "sl", split_axis=0, concat_axis=2, tiled=True)[0]
    far = shifted(kv_packed[:2], "sh", 1)
    grad_g, kv_packed = lax.optimization_barrier((grad_g, kv_packed))
    grad_g = lax.all_to_all(grad_g, ("sl", "head"), split_axis=0, concat_axis=2, tiled=True)[0]
    key_own = kv_packed[0]
    value_own = kv_packed[1]
    side_g = kv_packed[2]
    tokens = key_own.shape[0]
    logsum_g = join_three(side_g[:, : 3 * heads_here].reshape(tokens, heads_here, 3)).T
    start_g = jnp.round(join_three(side_g[:, 3 * heads_here : 3 * heads_here + 3])).astype(
        jnp.int32
    )
    qf_packed = jnp.concatenate(
        [
            queries.reshape(local_tokens, ring, heads_here, depth).transpose(1, 2, 0, 3),
            forward_out.reshape(local_tokens, ring, heads_here, depth).transpose(1, 2, 0, 3),
        ],
        axis=1,
    )
    qf_packed = lax.all_to_all(qf_packed, "sl", split_axis=0, concat_axis=2, tiled=True)[0]
    query_g = qf_packed[:heads_here]
    forward_g = qf_packed[heads_here:]
    delta_g = jnp.einsum("gtd,gtd->gt", forward_g, grad_g, preferred_element_type=jnp.float32)
    base = lax.axis_index("sh") * tokens
    start_rel = (start_g - base + WINDOW_LENGTH)[None, :]
    query_far, key_far = band_part(
        True, query_g, grad_g, logsum_g, delta_g, start_rel, far[0], far[1]
    )
    back = shifted(key_far, "sh", -1)
    query_g, key_far = lax.optimization_barrier((query_g, key_far))
    query_grad, key_sum, value_sum = band_part(
        False, query_g, grad_g, logsum_g, delta_g, start_rel, key_own, value_own, query_far
    )
    query_grad = query_grad.transpose(1, 0, 2)

    def to_tokens(x):
        items = x.shape[1]
        x = lax.all_to_all(x, ("sl", "head"), split_axis=0, concat_axis=1, tiled=True)
        rows_out = x.shape[0]
        return x.reshape(rows_out, ring, head_size, items, depth).transpose(0, 2, 1, 3, 4)

    key_total = key_sum + back[0].astype(jnp.float32)
    value_total = value_sum + back[1].astype(jnp.float32)
    key_grad = (key_total * score_scale).astype(jnp.bfloat16)[:, None]
    value_grad = value_total.astype(jnp.bfloat16)[:, None]
    outs = to_tokens(jnp.concatenate([query_grad, key_grad, value_grad], axis=1))
    rows_out = outs.shape[0]
    query_out = outs[:, :, :, :heads_here].reshape(rows_out, -1, depth)
    key_out = outs[:, :, :, heads_here].reshape(rows_out, -1, depth)
    value_out = outs[:, :, :, heads_here + 1].reshape(rows_out, -1, depth)
    return query_out, key_out, value_out


def solution(mesh):
    head, seq = mesh.devices.shape
    ring = WINDOW_LENGTH // BLOCK
    grouped = Mesh(mesh.devices.reshape(head, seq // ring, ring), ("head", "sh", "sl"))
    seq_axes = ("sh", "sl")
    placed = (
        P(seq_axes, "head", None),
        P(seq_axes, "head", None),
        P(seq_axes, "head", None),
        P(seq_axes, "head", None),
        P(seq_axes + ("head",), None, None),
        P("head", seq_axes),
        P(seq_axes),
    )
    out = P(seq_axes + ("head",), None, None)
    return jax.shard_map(
        on_device,
        mesh=grouped,
        in_specs=placed,
        out_specs=(out, out, out),
        check_vma=False,
    )
```
